128 devices in a mesh: ctx: 64 (over x, y_lo, z, core), tp: 2 (over y_hi).
Axes of the slice: x: 4, y: 4 (y_hi: 2, y_lo: 2; y = y_hi * 2 + y_lo), z: 4, core: 2. Of those that a mesh axis runs over, the one named last changes fastest.
Arguments:
- rotated_queries: bfloat16 [8192, 2048], P('ctx', 'tp'), may hold values from -150 to 150
- rotated_keys: bfloat16 [8192, 1024], P('ctx', 'tp'), may hold values from -5 to 5
- value_matrix: bfloat16 [8192, 1024], P('ctx', 'tp'), may hold values from -6 to 6
- out_grad: bfloat16 [8192, 5376], P('ctx', 'tp'), may hold values from -16 to 16
- out_weight: bfloat16 [2048, 5376], P('tp', 'ctx'), may hold values from -0.125 to 0.125
Outputs:
- query_grad: bfloat16 [8192, 2048], P('ctx', 'tp')
- key_gradient: bfloat16 [8192, 1024], P('ctx', 'tp')
- value_gradient: bfloat16 [8192, 1024], P('ctx', 'tp')
- weight_grad: float32 [2048, 5376], P('tp', 'ctx')
The draws below stay inside these ranges and needn't reach their ends.
All inputs are finite; a program needn't handle non-finite values.
Results may differ from the reference program's by a relative error of at most 0.013.
The reference program's roundings to bfloat16 on the way count: a program that leaves them out, or rounds other values in their place, can miss the bound.
Values may be sent and summed in bfloat16 or wider, within the bound.
No kernel may reach another device: no remote copies, remote signals or barrier semaphores. Data moves between devices by JAX's collectives and lax.ppermute only.
A program may use at most 128 MiB of HBM per device.

```python
import jax
import jax.numpy as jnp
from jax import lax

D = 5376
HEAD_SIZE = 128
WINDOW_SPAN = 1024
QUERY_HEAD_COUNT = 16
KEY_VALUE_HEADS = 8
TOK_DEV = 128
TOKEN_COUNT = 8192


def drawn_pair(key):
    group_width = QUERY_HEAD_COUNT // KEY_VALUE_HEADS
    starting_keys = jnp.clip(jax.random.normal(jax.random.fold_in(key, 11), (TOKEN_COUNT, KEY_VALUE_HEADS, HEAD_SIZE), jnp.float32), -5.0, 5.0)
    starting_query = jnp.clip(jax.random.normal(jax.random.fold_in(key, 12), (TOKEN_COUNT, KEY_VALUE_HEADS, group_width, HEAD_SIZE), jnp.float32), -5.0, 5.0)
    closing_keys = starting_keys
    final_query = starting_query
    return (final_query, closing_keys)


def draw_rotated_queries(key, part):
    final_query, closing_keys = drawn_pair(key)
    return final_query.reshape(TOKEN_COUNT, QUERY_HEAD_COUNT * HEAD_SIZE).astype(jnp.bfloat16)


def draw_rotated_keys(key, part):
    final_query, closing_keys = drawn_pair(key)
    return closing_keys.reshape(TOKEN_COUNT, KEY_VALUE_HEADS * HEAD_SIZE).astype(jnp.bfloat16)


def spiked(drawn, own_key, source, target, parts, factor):
    def block_of(position):
        return (jnp.arange(drawn.shape[position]) // (drawn.shape[position] // parts)).reshape((-1,) + (1,) * (drawn.ndim - 1 - position))

    first = jax.random.permutation(own_key, parts)[block_of(target)]
    second = (block_of(target) + parts // 2) % parts
    return jnp.where((block_of(source) == first) | (block_of(source) == second), factor * drawn, drawn)


def level_of(stream_key, shape, cuts, least, top_value):
    loudness, own = 1.0, jax.random.fold_in(stream_key, 6)
    for position, shards_of in cuts:
        draws = jnp.exp(jax.random.uniform(jax.random.fold_in(own, position), (shards_of,), jnp.float32, least / len(cuts), top_value / len(cuts)))
        loudness = loudness * jnp.repeat(draws, shape[position] // shards_of).reshape([-1 if axis == position else 1 for axis in range(len(shape))])
    return loudness


def normal_values(own_key, shape, spread, bound, cuts=(), held_as=jnp.bfloat16):
    drawn = jax.random.normal(own_key, shape, jnp.float32) * spread
    if len(cuts) > 0:
        drawn = level_of(own_key, shape, cuts, -0.22, 0.18) * drawn
    return jnp.clip(drawn, min=-bound, max=bound).astype(held_as)


def bell_draw_with(key, extent, width, most, pieces, heavy, kind=jnp.bfloat16):
    values = width * jax.random.normal(key, extent, jnp.float32)
    if pieces:
        values = values * level_of(key, extent, pieces, -0.22, 0.18)
    return jnp.clip(spiked(values, jax.random.fold_in(key, 3), *heavy), -most, most).astype(kind)


def setup_inputs(seed: int = 0) -> dict:
    streams_of = jax.random.split(jax.random.key(seed), 6)
    return {
        "rotated_queries": draw_rotated_queries(jax.random.fold_in(streams_of[5], 71), 0),
        "rotated_keys": draw_rotated_keys(jax.random.fold_in(streams_of[5], 71), 0),
        "value_matrix": normal_values(streams_of[2], (TOKEN_COUNT, KEY_VALUE_HEADS * HEAD_SIZE), 1.0, 6.0, ((0, 64), (1, 2))),
        "out_grad": bell_draw_with(streams_of[3], (TOKEN_COUNT, D), 1.0, 16.0, ((0, 64), (1, 2)), (0, 1, 64, 4.0)),
        "out_weight": normal_values(streams_of[4], (QUERY_HEAD_COUNT * HEAD_SIZE, D), (QUERY_HEAD_COUNT * HEAD_SIZE) ** -0.5, 0.125, ((0, 2), (1, 64))),
    }


score_scale = 168.0 ** -0.5


def reference(rotated_queries, rotated_keys, value_matrix, out_grad, out_weight):
    group_width = QUERY_HEAD_COUNT // KEY_VALUE_HEADS
    query_vector = rotated_queries.reshape(TOKEN_COUNT, KEY_VALUE_HEADS, group_width, HEAD_SIZE)
    padding_rows = jnp.zeros((WINDOW_SPAN, KEY_VALUE_HEADS * HEAD_SIZE), jnp.bfloat16)
    keyed_result = jnp.concatenate([padding_rows, rotated_keys], 0).reshape(TOKEN_COUNT + WINDOW_SPAN, KEY_VALUE_HEADS, HEAD_SIZE)
    valued_result = jnp.concatenate([padding_rows, value_matrix], 0).reshape(TOKEN_COUNT + WINDOW_SPAN, KEY_VALUE_HEADS, HEAD_SIZE)
    blocks = TOKEN_COUNT // TOK_DEV
    span = WINDOW_SPAN + TOK_DEV

    def block_inputs(index):
        first = (index * TOK_DEV).astype(jnp.int32)
        query_block = lax.dynamic_slice_in_dim(query_vector, first, TOK_DEV, 0).astype(jnp.float32)
        key_block = lax.dynamic_slice_in_dim(keyed_result, first, span, 0).astype(jnp.float32)
        value_block = lax.dynamic_slice_in_dim(valued_result, first, span, 0).astype(jnp.float32)
        query_pos = first + jnp.arange(TOK_DEV, dtype=jnp.int32)
        key_pos = first - WINDOW_SPAN + jnp.arange(span, dtype=jnp.int32)
        allowed = (key_pos[None, :] <= query_pos[:, None]) & (query_pos[:, None] - key_pos[None, :] < WINDOW_SPAN) & (key_pos[None, :] >= 0)
        scores = jnp.einsum("thgd,khd->hgtk", query_block, key_block, precision=lax.Precision.HIGHEST) * score_scale
        scores = jnp.where(allowed[None, None], scores, -jnp.inf)
        return first, query_block, key_block, value_block, scores

    def forward_block(index):
        first, query_block, key_block, value_block, scores = block_inputs(index)
        row_max = jnp.max(scores, axis=-1, keepdims=True)
        log_total = row_max + jnp.log(jnp.sum(jnp.exp(scores - row_max), axis=-1, keepdims=True))
        probs = jnp.exp(scores - log_total).astype(jnp.bfloat16)
        output = jnp.einsum("hgtk,khd->thgd", probs.astype(jnp.float32), value_block, precision=lax.Precision.HIGHEST)
        return output.astype(jnp.bfloat16).reshape(TOK_DEV, QUERY_HEAD_COUNT * HEAD_SIZE), log_total[..., 0]

    attn_blocks, totals = lax.map(forward_block, jnp.arange(blocks, dtype=jnp.int32))
    attention_probs = attn_blocks.reshape(TOKEN_COUNT, QUERY_HEAD_COUNT * HEAD_SIZE)
    attention_gradient = jnp.dot(out_grad, out_weight.T, preferred_element_type=jnp.float32).astype(jnp.bfloat16)
    weight_grad = jnp.dot(attention_probs.T, out_grad, preferred_element_type=jnp.float32) * (TOKEN_COUNT ** -0.5)
    row_deltas = jnp.sum(attention_gradient.reshape(TOKEN_COUNT, KEY_VALUE_HEADS, group_width, HEAD_SIZE).astype(jnp.float32) * attention_probs.reshape(TOKEN_COUNT, KEY_VALUE_HEADS, group_width, HEAD_SIZE).astype(jnp.float32), axis=-1)
    head_gradients = attention_gradient.reshape(TOKEN_COUNT, KEY_VALUE_HEADS, group_width, HEAD_SIZE)

    def backward_block(carry, index):
        key_accumulator, value_accumulator = carry
        first, query_block, key_block, value_block, scores = block_inputs(index)
        log_total = totals[index]
        delta_block = lax.dynamic_slice_in_dim(row_deltas, first, TOK_DEV, 0)
        grad_block = lax.dynamic_slice_in_dim(head_gradients, first, TOK_DEV, 0).astype(jnp.float32)
        probs = jnp.exp(scores - log_total[..., None])
        probs_low = probs.astype(jnp.bfloat16).astype(jnp.float32)
        prob_grad = jnp.einsum("thgd,khd->hgtk", grad_block, value_block, precision=lax.Precision.HIGHEST)
        delta_hgt = jnp.transpose(delta_block, (1, 2, 0))
        score_grad = (probs * (prob_grad - delta_hgt[..., None])).astype(jnp.bfloat16).astype(jnp.float32)
        query_part = jnp.einsum("hgtk,khd->thgd", score_grad, key_block, precision=lax.Precision.HIGHEST) * score_scale
        key_part = jnp.einsum("hgtk,thgd->khd", score_grad, query_block, precision=lax.Precision.HIGHEST) * score_scale
        value_part = jnp.einsum("hgtk,thgd->khd", probs_low, grad_block, precision=lax.Precision.HIGHEST)
        key_accumulator = lax.dynamic_update_slice_in_dim(key_accumulator, lax.dynamic_slice_in_dim(key_accumulator, first, span, 0) + key_part, first, 0)
        value_accumulator = lax.dynamic_update_slice_in_dim(value_accumulator, lax.dynamic_slice_in_dim(value_accumulator, first, span, 0) + value_part, first, 0)
        return (key_accumulator, value_accumulator), query_part.astype(jnp.bfloat16).reshape(TOK_DEV, QUERY_HEAD_COUNT * HEAD_SIZE)

    empty_accumulator = jnp.zeros((TOKEN_COUNT + WINDOW_SPAN, KEY_VALUE_HEADS, HEAD_SIZE), jnp.float32)
    (key_accumulator, value_accumulator), query_blocks = lax.scan(backward_block, (empty_accumulator, empty_accumulator), jnp.arange(blocks, dtype=jnp.int32))
    query_grad = query_blocks.reshape(TOKEN_COUNT, QUERY_HEAD_COUNT * HEAD_SIZE)
    key_gradient = key_accumulator[WINDOW_SPAN:].reshape(TOKEN_COUNT, KEY_VALUE_HEADS * HEAD_SIZE).astype(jnp.bfloat16)
    value_gradient = value_accumulator[WINDOW_SPAN:].reshape(TOKEN_COUNT, KEY_VALUE_HEADS * HEAD_SIZE).astype(jnp.bfloat16)
    return (query_grad, key_gradient, value_gradient, weight_grad)
```

```python
import jax
import jax.numpy as jnp
from jax import lax
from jax.sharding import PartitionSpec as P

HEAD_SIZE = 128
WINDOW_SPAN = 1024
QUERY_HEAD_COUNT = 16
KEY_VALUE_HEADS = 8


score_scale = 168.0 ** (-0.5)


def from_behind(block, axis, distance):
    devices = range(lax.axis_size(axis))
    route = [(i - distance, i) for i in devices if i - distance in devices]
    return lax.ppermute(block, axis, route)


def band_mask(query_pos, key_pos):
    earlier = key_pos[None, :] <= query_pos[:, None]
    within = query_pos[:, None] - key_pos[None, :] < WINDOW_SPAN
    return earlier & within & (key_pos[None, :] >= 0)


def scores_for(query_head, key_head, allowed):
    scaled = (
        jnp.einsum("tgd,kd->gtk", query_head, key_head, preferred_element_type=jnp.float32)
        * score_scale
    )
    return jnp.where(allowed[None], scaled, -jnp.inf)


def forward_head(query_head, key_head, value_head, allowed):
    scores = scores_for(query_head, key_head, allowed)
    row_max = jnp.max(scores, axis=-1, keepdims=True)
    log_total = row_max + jnp.log(jnp.sum(jnp.exp(scores - row_max), axis=-1, keepdims=True))
    probs = jnp.exp(scores - log_total).astype(jnp.bfloat16)
    output = jnp.einsum("gtk,kd->tgd", probs, value_head, preferred_element_type=jnp.float32)
    return (output.astype(jnp.bfloat16), log_total[..., 0])


def grad_band(query_head, grad_head, log_total, delta_head, key_head, value_head, allowed):
    scores = scores_for(query_head, key_head, allowed)
    probs = jnp.exp(scores - log_total[..., None])
    probs_low = probs.astype(jnp.bfloat16)
    prob_grad = jnp.einsum("tgd,kd->gtk", grad_head, value_head, preferred_element_type=jnp.float32)
    score_grad = (probs * (prob_grad - delta_head.T[..., None])).astype(jnp.bfloat16)
    query_part = (
        jnp.einsum("gtk,kd->tgd", score_grad, key_head, preferred_element_type=jnp.float32)
        * score_scale
    )
    key_part = (
        jnp.einsum("gtk,tgd->kd", score_grad, query_head, preferred_element_type=jnp.float32)
        * score_scale
    )
    value_part = jnp.einsum("gtk,tgd->kd", probs_low, grad_head, preferred_element_type=jnp.float32)
    return (query_part, key_part, value_part)


def per_device(rotated_queries, rotated_keys, value_matrix, out_grad, out_weight):
    tokens_dev = rotated_queries.shape[0]
    n_ctx = lax.axis_size(("cg", "cp"))
    kv_local = rotated_keys.shape[1] // HEAD_SIZE
    group_width = QUERY_HEAD_COUNT // KEY_VALUE_HEADS
    reach_count = WINDOW_SPAN // tokens_dev
    start_pos = lax.axis_index(("cg", "cp")) * tokens_dev
    query_pos = start_pos + jnp.arange(tokens_dev, dtype=jnp.int32)
    earlier = []
    for offset in range(reach_count, 0, -1):
        earlier.append(from_behind((rotated_keys, value_matrix), ("cg", "cp"), offset))
    key_ext = jnp.concatenate([pair[0] for pair in earlier] + [rotated_keys], 0)
    value_ext = jnp.concatenate([pair[1] for pair in earlier] + [value_matrix], 0)
    key_pos = (
        start_pos
        - reach_count * tokens_dev
        + jnp.arange((reach_count + 1) * tokens_dev, dtype=jnp.int32)
    )
    full_mask = band_mask(query_pos, key_pos)
    query_heads = rotated_queries.reshape(tokens_dev, kv_local, group_width, HEAD_SIZE).transpose(
        1, 0, 2, 3
    )
    key_heads = key_ext.reshape(-1, kv_local, HEAD_SIZE).transpose(1, 0, 2)
    value_heads = value_ext.reshape(-1, kv_local, HEAD_SIZE).transpose(1, 0, 2)
    attn_heads, log_totals = lax.map(
        lambda items: forward_head(items[0], items[1], items[2], full_mask),
        (query_heads, key_heads, value_heads),
    )
    attn_rows = attn_heads.transpose(1, 0, 2, 3)
    attention_probs = attn_rows.reshape(tokens_dev, -1)
    cotangent = lax.all_gather(out_grad, "tp", axis=1, tiled=True)
    grad_sum = lax.dot_general(
        cotangent,
        lax.all_gather(out_weight, ("cg", "cp"), axis=1, tiled=True),
        (((1,), (1,)), ((), ())),
        preferred_element_type=jnp.float32,
    )
    attention_gradient = grad_sum.astype(jnp.bfloat16)
    group_size = lax.axis_size("cp")
    group_count = lax.axis_size("cg")
    block = cotangent.shape[1] // n_ctx
    by_position = cotangent.reshape(tokens_dev, group_count, group_size, block).transpose(0, 2, 1, 3)
    group_cotangent = lax.all_to_all(by_position, "cp", 1, 0, tiled=True).reshape(
        group_size * tokens_dev, group_count, block
    )
    group_probs = lax.all_gather(attention_probs, "cp", axis=0, tiled=True)
    weight_term = jnp.einsum(
        "th,tak->ahk", group_probs, group_cotangent, preferred_element_type=jnp.float32
    ) * (tokens_dev * n_ctx) ** (-0.5)
    weight_grad = lax.psum_scatter(weight_term, "cg", scatter_dimension=0, tiled=True)[0]
    grad_rows = attention_gradient.reshape(tokens_dev, kv_local, group_width, HEAD_SIZE)
    row_deltas = jnp.sum(grad_rows.astype(jnp.float32) * attn_rows.astype(jnp.float32), axis=-1)
    head_gradients = grad_rows.transpose(1, 0, 2, 3)
    delta_heads = row_deltas.transpose(1, 0, 2)
    query_parts, key_parts, value_parts = lax.map(
        lambda items: grad_band(
            items[0], items[1], items[2], items[3], items[4], items[5], full_mask
        ),
        (query_heads, head_gradients, log_totals, delta_heads, key_heads, value_heads),
    )
    key_ext_grad = key_parts.transpose(1, 0, 2).reshape(-1, kv_local * HEAD_SIZE)
    value_ext_grad = value_parts.transpose(1, 0, 2).reshape(-1, kv_local * HEAD_SIZE)
    key_total = key_ext_grad[reach_count * tokens_dev :]
    value_total = value_ext_grad[reach_count * tokens_dev :]
    for offset in range(1, reach_count + 1):
        first_row = (reach_count - offset) * tokens_dev
        back_key, back_value = from_behind(
            (
                key_ext_grad[first_row : first_row + tokens_dev],
                value_ext_grad[first_row : first_row + tokens_dev],
            ),
            ("cg", "cp"),
            -offset,
        )
        key_total = key_total + back_key
        value_total = value_total + back_value
    query_grad = query_parts.transpose(1, 0, 2, 3).reshape(tokens_dev, -1).astype(jnp.bfloat16)
    return (
        query_grad,
        key_total.astype(jnp.bfloat16),
        value_total.astype(jnp.bfloat16),
        weight_grad,
    )


GROUP_SIZE = 8


def solution(mesh):
    n_ctx = mesh.shape["ctx"]
    group_size = GROUP_SIZE if n_ctx % GROUP_SIZE == 0 else 1
    devices = mesh.devices.reshape(n_ctx // group_size, group_size, mesh.shape["tp"])
    grouped = jax.sharding.Mesh(devices, ("cg", "cp", "tp"))
    ctx = ("cg", "cp")
    placed = (P(ctx, "tp"), P(ctx, "tp"), P(ctx, "tp"), P(ctx, "tp"), P("tp", ctx))
    return jax.shard_map(
        per_device,
        mesh=grouped,
        in_specs=placed,
        out_specs=(P(ctx, "tp"), P(ctx, "tp"), P(ctx, "tp"), P("tp", ctx)),
        check_vma=False,
    )
```

```python
import jax
import jax.numpy as jnp
from jax import lax
from jax.sharding import PartitionSpec as P

HEAD_SIZE = 128
WINDOW_SPAN = 1024
QUERY_HEAD_COUNT = 16
KEY_VALUE_HEADS = 8


score_scale = 168.0 ** (-0.5)


def from_behind(block, axis, distance):
    devices = range(lax.axis_size(axis))
    route = [(i - distance, i) for i in devices if i - distance in devices]
    return lax.ppermute(block, axis, route)


def band_mask(query_pos, key_pos):
    earlier = key_pos[None, :] <= query_pos[:, None]
    within = query_pos[:, None] - key_pos[None, :] < WINDOW_SPAN
    return earlier & within & (key_pos[None, :] >= 0)


def scores_for(query_head, key_head, allowed):
    scaled = (
        jnp.einsum("tgd,kd->gtk", query_head, key_head, preferred_element_type=jnp.float32)
        * score_scale
    )
    return jnp.where(allowed[None], scaled, -jnp.inf)


def forward_head(query_head, key_head, value_head, allowed):
    scores = scores_for(query_head, key_head, allowed)
    row_max = jnp.max(scores, axis=-1, keepdims=True)
    log_total = row_max + jnp.log(jnp.sum(jnp.exp(scores - row_max), axis=-1, keepdims=True))
    probs = jnp.exp(scores - log_total).astype(jnp.bfloat16)
    output = jnp.einsum("gtk,kd->tgd", probs, value_head, preferred_element_type=jnp.float32)
    return (output.astype(jnp.bfloat16), log_total[..., 0])


def grad_band(query_head, grad_head, log_total, delta_head, key_head, value_head, allowed):
    scores = scores_for(query_head, key_head, allowed)
    probs = jnp.exp(scores - log_total[..., None])
    probs_low = probs.astype(jnp.bfloat16)
    prob_grad = jnp.einsum("tgd,kd->gtk", grad_head, value_head, preferred_element_type=jnp.float32)
    score_grad = (probs * (prob_grad - delta_head.T[..., None])).astype(jnp.bfloat16)
    query_part = (
        jnp.einsum("gtk,kd->tgd", score_grad, key_head, preferred_element_type=jnp.float32)
        * score_scale
    )
    key_part = (
        jnp.einsum("gtk,tgd->kd", score_grad, query_head, preferred_element_type=jnp.float32)
        * score_scale
    )
    value_part = jnp.einsum("gtk,tgd->kd", probs_low, grad_head, preferred_element_type=jnp.float32)
    return (query_part, key_part, value_part)


def per_device(rotated_queries, rotated_keys, value_matrix, out_grad, out_weight):
    tokens_dev = rotated_queries.shape[0]
    n_ctx = lax.axis_size(("cg", "cp"))
    kv_local = rotated_keys.shape[1] // HEAD_SIZE
    group_width = QUERY_HEAD_COUNT // KEY_VALUE_HEADS
    reach_count = WINDOW_SPAN // tokens_dev
    start_pos = lax.axis_index(("cg", "cp")) * tokens_dev
    query_pos = start_pos + jnp.arange(tokens_dev, dtype=jnp.int32)
    earlier = []
    for offset in range(reach_count, 0, -1):
        earlier.append(from_behind((rotated_keys, value_matrix), ("cg", "cp"), offset))
    key_ext = jnp.concatenate([pair[0] for pair in earlier] + [rotated_keys], 0)
    value_ext = jnp.concatenate([pair[1] for pair in earlier] + [value_matrix], 0)
    key_pos = (
        start_pos
        - reach_count * tokens_dev
        + jnp.arange((reach_count + 1) * tokens_dev, dtype=jnp.int32)
    )
    full_mask = band_mask(query_pos, key_pos)
    query_heads = rotated_queries.reshape(tokens_dev, kv_local, group_width, HEAD_SIZE).transpose(
        1, 0, 2, 3
    )
    key_heads = key_ext.reshape(-1, kv_local, HEAD_SIZE).transpose(1, 0, 2)
    value_heads = value_ext.reshape(-1, kv_local, HEAD_SIZE).transpose(1, 0, 2)
    attn_heads, log_totals = lax.map(
        lambda items: forward_head(items[0], items[1], items[2], full_mask),
        (query_heads, key_heads, value_heads),
    )
    attn_rows = attn_heads.transpose(1, 0, 2, 3)
    attention_probs = attn_rows.reshape(tokens_dev, -1)
    partner_grad = lax.ppermute(out_grad, "tp", [(0, 1), (1, 0)])
    cotangent = jnp.where(
        lax.axis_index("tp") == 0,
        jnp.concatenate([out_grad, partner_grad], 1),
        jnp.concatenate([partner_grad, out_grad], 1),
    )
    grad_sum = lax.dot_general(
        cotangent,
        lax.all_gather(out_weight, ("cg", "cp"), axis=1, tiled=True),
        (((1,), (1,)), ((), ())),
        preferred_element_type=jnp.float32,
    )
    attention_gradient = grad_sum.astype(jnp.bfloat16)
    group_size = lax.axis_size("cp")
    group_count = lax.axis_size("cg")
    block = cotangent.shape[1] // n_ctx
    by_position = cotangent.reshape(tokens_dev, group_count, group_size, block).transpose(2, 0, 1, 3)
    heads_width = attention_probs.shape[1]
    outgoing = jnp.concatenate(
        [
            jnp.broadcast_to(attention_probs, (group_size,) + attention_probs.shape),
            by_position.reshape(group_size, tokens_dev, group_count * block),
        ],
        2,
    )
    incoming = lax.all_to_all(outgoing, "cp", 0, 0, tiled=True)
    group_probs = incoming[:, :, :heads_width].reshape(group_size * tokens_dev, heads_width)
    group_cotangent = incoming[:, :, heads_width:].reshape(
        group_size * tokens_dev, group_count, block
    )
    weight_term = jnp.einsum(
        "th,tak->ahk", group_probs, group_cotangent, preferred_element_type=jnp.float32
    ) * (tokens_dev * n_ctx) ** (-0.5)
    weight_grad = lax.psum_scatter(weight_term, "cg", scatter_dimension=0, tiled=True)[0]
    grad_rows = attention_gradient.reshape(tokens_dev, kv_local, group_width, HEAD_SIZE)
    row_deltas = jnp.sum(grad_rows.astype(jnp.float32) * attn_rows.astype(jnp.float32), axis=-1)
    head_gradients = grad_rows.transpose(1, 0, 2, 3)
    delta_heads = row_deltas.transpose(1, 0, 2)
    query_parts, key_parts, value_parts = lax.map(
        lambda items: grad_band(
            items[0], items[1], items[2], items[3], items[4], items[5], full_mask
        ),
        (query_heads, head_gradients, log_totals, delta_heads, key_heads, value_heads),
    )
    key_ext_grad = key_parts.transpose(1, 0, 2).reshape(-1, kv_local * HEAD_SIZE)
    value_ext_grad = value_parts.transpose(1, 0, 2).reshape(-1, kv_local * HEAD_SIZE)
    key_total = key_ext_grad[reach_count * tokens_dev :]
    value_total = value_ext_grad[reach_count * tokens_dev :]
    for offset in range(1, reach_count + 1):
        first_row = (reach_count - offset) * tokens_dev
        back_key, back_value = from_behind(
            (
                key_ext_grad[first_row : first_row + tokens_dev],
                value_ext_grad[first_row : first_row + tokens_dev],
            ),
            ("cg", "cp"),
            -offset,
        )
        key_total = key_total + back_key
        value_total = value_total + back_value
    query_grad = query_parts.transpose(1, 0, 2, 3).reshape(tokens_dev, -1).astype(jnp.bfloat16)
    return (
        query_grad,
        key_total.astype(jnp.bfloat16),
        value_total.astype(jnp.bfloat16),
        weight_grad,
    )


GROUP_SIZE = 8


def solution(mesh):
    n_ctx = mesh.shape["ctx"]
    group_size = GROUP_SIZE if n_ctx % GROUP_SIZE == 0 else 1
    devices = mesh.devices.reshape(n_ctx // group_size, group_size, mesh.shape["tp"])
    grouped = jax.sharding.Mesh(devices, ("cg", "cp", "tp"))
    ctx = ("cg", "cp")
    placed = (P(ctx, "tp"), P(ctx, "tp"), P(ctx, "tp"), P(ctx, "tp"), P("tp", ctx))
    return jax.shard_map(
        per_device,
        mesh=grouped,
        in_specs=placed,
        out_specs=(P(ctx, "tp"), P(ctx, "tp"), P(ctx, "tp"), P("tp", ctx)),
        check_vma=False,
    )
```

```python
import jax
import jax.numpy as jnp
from jax import lax
from jax.sharding import PartitionSpec as P

HEAD_SIZE = 128
WINDOW_SPAN = 1024
QUERY_HEAD_COUNT = 16
KEY_VALUE_HEADS = 8


score_scale = 168.0 ** (-0.5)


def from_behind(block, axis, distance):
    devices = range(lax.axis_size(axis))
    route = [(i - distance, i) for i in devices if i - distance in devices]
    return lax.ppermute(block, axis, route)


def band_mask(query_pos, key_pos):
    earlier = key_pos[None, :] <= query_pos[:, None]
    within = query_pos[:, None] - key_pos[None, :] < WINDOW_SPAN
    return earlier & within & (key_pos[None, :] >= 0)


def scores_for(query_head, key_head, allowed):
    scaled = (
        jnp.einsum("tgd,kd->gtk", query_head, key_head, preferred_element_type=jnp.float32)
        * score_scale
    )
    return jnp.where(allowed[None], scaled, -jnp.inf)


def forward_head(query_head, key_head, value_head, allowed):
    scores = scores_for(query_head, key_head, allowed)
    row_max = jnp.max(scores, axis=-1, keepdims=True)
    log_total = row_max + jnp.log(jnp.sum(jnp.exp(scores - row_max), axis=-1, keepdims=True))
    probs = jnp.exp(scores - log_total).astype(jnp.bfloat16)
    output = jnp.einsum("gtk,kd->tgd", probs, value_head, preferred_element_type=jnp.float32)
    return (output.astype(jnp.bfloat16), log_total[..., 0])


def grad_band(query_head, grad_head, log_total, delta_head, key_head, value_head, allowed):
    scores = scores_for(query_head, key_head, allowed)
    probs = jnp.exp(scores - log_total[..., None])
    probs_low = probs.astype(jnp.bfloat16)
    prob_grad = jnp.einsum("tgd,kd->gtk", grad_head, value_head, preferred_element_type=jnp.float32)
    score_grad = (probs * (prob_grad - delta_head.T[..., None])).astype(jnp.bfloat16)
    query_part = (
        jnp.einsum("gtk,kd->tgd", score_grad, key_head, preferred_element_type=jnp.float32)
        * score_scale
    )
    key_part = (
        jnp.einsum("gtk,tgd->kd", score_grad, query_head, preferred_element_type=jnp.float32)
        * score_scale
    )
    value_part = jnp.einsum("gtk,tgd->kd", probs_low, grad_head, preferred_element_type=jnp.float32)
    return (query_part, key_part, value_part)


def per_device(rotated_queries, rotated_keys, value_matrix, out_grad, out_weight):
    tokens_dev = rotated_queries.shape[0]
    n_ctx = lax.axis_size(("cg", "cp"))
    kv_local = rotated_keys.shape[1] // HEAD_SIZE
    group_width = QUERY_HEAD_COUNT // KEY_VALUE_HEADS
    reach_count = WINDOW_SPAN // tokens_dev
    start_pos = lax.axis_index(("cg", "cp")) * tokens_dev
    query_pos = start_pos + jnp.arange(tokens_dev, dtype=jnp.int32)
    kv_width = rotated_keys.shape[1]
    own_pair = jnp.concatenate([rotated_keys, value_matrix], 1)
    earlier = [from_behind(own_pair, ("cg", "cp"), offset) for offset in range(reach_count, 0, -1)]
    pair_ext = jnp.concatenate(earlier + [own_pair], 0)
    key_ext = pair_ext[:, :kv_width]
    value_ext = pair_ext[:, kv_width:]
    key_pos = (
        start_pos
        - reach_count * tokens_dev
        + jnp.arange((reach_count + 1) * tokens_dev, dtype=jnp.int32)
    )
    full_mask = band_mask(query_pos, key_pos)
    query_heads = rotated_queries.reshape(tokens_dev, kv_local, group_width, HEAD_SIZE).transpose(
        1, 0, 2, 3
    )
    key_heads = key_ext.reshape(-1, kv_local, HEAD_SIZE).transpose(1, 0, 2)
    value_heads = value_ext.reshape(-1, kv_local, HEAD_SIZE).transpose(1, 0, 2)
    attn_heads, log_totals = lax.map(
        lambda items: forward_head(items[0], items[1], items[2], full_mask),
        (query_heads, key_heads, value_heads),
    )
    attn_rows = attn_heads.transpose(1, 0, 2, 3)
    attention_probs = attn_rows.reshape(tokens_dev, -1)
    partner_grad = lax.ppermute(out_grad, "tp", [(0, 1), (1, 0)])
    cotangent = jnp.where(
        lax.axis_index("tp") == 0,
        jnp.concatenate([out_grad, partner_grad], 1),
        jnp.concatenate([partner_grad, out_grad], 1),
    )
    grad_sum = lax.dot_general(
        cotangent,
        lax.all_gather(out_weight, ("cg", "cp"), axis=1, tiled=True),
        (((1,), (1,)), ((), ())),
        preferred_element_type=jnp.float32,
    )
    attention_gradient = grad_sum.astype(jnp.bfloat16)
    group_size = lax.axis_size("cp")
    group_count = lax.axis_size("cg")
    block = cotangent.shape[1] // n_ctx
    by_position = cotangent.reshape(tokens_dev, group_count, group_size, block).transpose(2, 0, 1, 3)
    heads_width = attention_probs.shape[1]
    outgoing = jnp.concatenate(
        [
            jnp.broadcast_to(attention_probs, (group_size,) + attention_probs.shape),
            by_position.reshape(group_size, tokens_dev, group_count * block),
        ],
        2,
    )
    incoming = lax.all_to_all(outgoing, "cp", 0, 0, tiled=True)
    group_probs = incoming[:, :, :heads_width].reshape(group_size * tokens_dev, heads_width)
    group_cotangent = incoming[:, :, heads_width:].reshape(
        group_size * tokens_dev, group_count, block
    )
    weight_term = jnp.einsum(
        "th,tak->ahk", group_probs, group_cotangent, preferred_element_type=jnp.float32
    ) * (tokens_dev * n_ctx) ** (-0.5)
    weight_grad = lax.psum_scatter(weight_term, "cg", scatter_dimension=0, tiled=True)[0]
    grad_rows = attention_gradient.reshape(tokens_dev, kv_local, group_width, HEAD_SIZE)
    row_deltas = jnp.sum(grad_rows.astype(jnp.float32) * attn_rows.astype(jnp.float32), axis=-1)
    head_gradients = grad_rows.transpose(1, 0, 2, 3)
    delta_heads = row_deltas.transpose(1, 0, 2)
    query_parts, key_parts, value_parts = lax.map(
        lambda items: grad_band(
            items[0], items[1], items[2], items[3], items[4], items[5], full_mask
        ),
        (query_heads, head_gradients, log_totals, delta_heads, key_heads, value_heads),
    )
    key_ext_grad = key_parts.transpose(1, 0, 2).reshape(-1, kv_local * HEAD_SIZE)
    value_ext_grad = value_parts.transpose(1, 0, 2).reshape(-1, kv_local * HEAD_SIZE)
    pair_grad = jnp.concatenate([key_ext_grad, value_ext_grad], 1)
    pair_total = pair_grad[reach_count * tokens_dev :]
    for offset in range(1, reach_count + 1):
        first_row = (reach_count - offset) * tokens_dev
        sent = pair_grad[first_row : first_row + tokens_dev].astype(jnp.bfloat16)
        pair_total = pair_total + from_behind(sent, ("cg", "cp"), -offset).astype(jnp.float32)
    key_total = pair_total[:, :kv_width]
    value_total = pair_total[:, kv_width:]
    query_grad = query_parts.transpose(1, 0, 2, 3).reshape(tokens_dev, -1).astype(jnp.bfloat16)
    return (
        query_grad,
        key_total.astype(jnp.bfloat16),
        value_total.astype(jnp.bfloat16),
        weight_grad,
    )


GROUP_SIZE = 8


def solution(mesh):
    n_ctx = mesh.shape["ctx"]
    group_size = GROUP_SIZE if n_ctx % GROUP_SIZE == 0 else 1
    devices = mesh.devices.reshape(n_ctx // group_size, group_size, mesh.shape["tp"])
    grouped = jax.sharding.Mesh(devices, ("cg", "cp", "tp"))
    ctx = ("cg", "cp")
    placed = (P(ctx, "tp"), P(ctx, "tp"), P(ctx, "tp"), P(ctx, "tp"), P("tp", ctx))
    return jax.shard_map(
        per_device,
        mesh=grouped,
        in_specs=placed,
        out_specs=(P(ctx, "tp"), P(ctx, "tp"), P(ctx, "tp"), P("tp", ctx)),
        check_vma=False,
    )
```

```python
import jax
import jax.numpy as jnp
from jax import lax
from jax.sharding import PartitionSpec as P

HEAD_SIZE = 128
WINDOW_SPAN = 1024
QUERY_HEAD_COUNT = 16
KEY_VALUE_HEADS = 8


score_scale = 168.0 ** (-0.5)


def from_behind(block, axis, distance):
    devices = range(lax.axis_size(axis))
    route = [(i - distance, i) for i in devices if i - distance in devices]
    return lax.ppermute(block, axis, route)


def band_mask(query_pos, key_pos):
    earlier = key_pos[None, :] <= query_pos[:, None]
    within = query_pos[:, None] - key_pos[None, :] < WINDOW_SPAN
    return earlier & within & (key_pos[None, :] >= 0)


def scores_for(query_head, key_head, allowed):
    scaled = (
        jnp.einsum("tgd,kd->gtk", query_head, key_head, preferred_element_type=jnp.float32)
        * score_scale
    )
    return jnp.where(allowed[None], scaled, -jnp.inf)


def forward_head(query_head, key_head, value_head, allowed):
    scores = scores_for(query_head, key_head, allowed)
    row_max = jnp.max(scores, axis=-1, keepdims=True)
    log_total = row_max + jnp.log(jnp.sum(jnp.exp(scores - row_max), axis=-1, keepdims=True))
    probs = jnp.exp(scores - log_total).astype(jnp.bfloat16)
    output = jnp.einsum("gtk,kd->tgd", probs, value_head, preferred_element_type=jnp.float32)
    return (output.astype(jnp.bfloat16), log_total[..., 0])


def grad_band(query_head, grad_head, log_total, delta_head, key_head, value_head, allowed):
    scores = scores_for(query_head, key_head, allowed)
    probs = jnp.exp(scores - log_total[..., None])
    probs_low = probs.astype(jnp.bfloat16)
    prob_grad = jnp.einsum("tgd,kd->gtk", grad_head, value_head, preferred_element_type=jnp.float32)
    score_grad = (probs * (prob_grad - delta_head.T[..., None])).astype(jnp.bfloat16)
    query_part = (
        jnp.einsum("gtk,kd->tgd", score_grad, key_head, preferred_element_type=jnp.float32)
        * score_scale
    )
    key_part = (
        jnp.einsum("gtk,tgd->kd", score_grad, query_head, preferred_element_type=jnp.float32)
        * score_scale
    )
    value_part = jnp.einsum("gtk,tgd->kd", probs_low, grad_head, preferred_element_type=jnp.float32)
    return (query_part, key_part, value_part)


def per_device(rotated_queries, rotated_keys, value_matrix, out_grad, out_weight):
    tokens_dev = rotated_queries.shape[0]
    n_ctx = lax.axis_size(CTX)
    kv_local = rotated_keys.shape[1] // HEAD_SIZE
    group_width = QUERY_HEAD_COUNT // KEY_VALUE_HEADS
    reach_count = WINDOW_SPAN // tokens_dev
    start_pos = lax.axis_index(CTX) * tokens_dev
    query_pos = start_pos + jnp.arange(tokens_dev, dtype=jnp.int32)
    kv_width = rotated_keys.shape[1]
    own_pair = jnp.concatenate([rotated_keys, value_matrix], 1)
    earlier = [from_behind(own_pair, CTX, offset) for offset in range(reach_count, 0, -1)]
    pair_ext = jnp.concatenate(earlier + [own_pair], 0)
    key_ext = pair_ext[:, :kv_width]
    value_ext = pair_ext[:, kv_width:]
    key_pos = (
        start_pos
        - reach_count * tokens_dev
        + jnp.arange((reach_count + 1) * tokens_dev, dtype=jnp.int32)
    )
    full_mask = band_mask(query_pos, key_pos)
    query_heads = rotated_queries.reshape(tokens_dev, kv_local, group_width, HEAD_SIZE).transpose(
        1, 0, 2, 3
    )
    key_heads = key_ext.reshape(-1, kv_local, HEAD_SIZE).transpose(1, 0, 2)
    value_heads = value_ext.reshape(-1, kv_local, HEAD_SIZE).transpose(1, 0, 2)
    attn_heads, log_totals = lax.map(
        lambda items: forward_head(items[0], items[1], items[2], full_mask),
        (query_heads, key_heads, value_heads),
    )
    attn_rows = attn_heads.transpose(1, 0, 2, 3)
    attention_probs = attn_rows.reshape(tokens_dev, -1)
    partner_grad = lax.ppermute(out_grad, "tp", [(0, 1), (1, 0)])
    cotangent = jnp.where(
        lax.axis_index("tp") == 0,
        jnp.concatenate([out_grad, partner_grad], 1),
        jnp.concatenate([partner_grad, out_grad], 1),
    )
    chip_weights = lax.all_gather(out_weight, ("cg", "cz"), axis=0, tiled=False)
    core = lax.axis_index("core")
    by_core = cotangent.reshape(tokens_dev, n_ctx // 2, 2, -1)
    own_columns = lax.dynamic_index_in_dim(by_core, core, 2, keepdims=False)
    other_columns = lax.dynamic_index_in_dim(by_core, 1 - core, 2, keepdims=False)
    swap = [(0, 1), (1, 0)]
    partner_columns = lax.ppermute(other_columns, "core", swap)
    own_part = jnp.einsum(
        "tbk,bhk->th", own_columns, chip_weights, preferred_element_type=jnp.float32
    )
    partner_part = jnp.einsum(
        "tbk,bhk->th", partner_columns, chip_weights, preferred_element_type=jnp.float32
    )
    grad_sum = own_part + lax.ppermute(partner_part, "core", swap)
    attention_gradient = grad_sum.astype(jnp.bfloat16)
    group_size = lax.axis_size(GROUP)
    group_count = lax.axis_size("cg")
    block = cotangent.shape[1] // n_ctx
    by_position = cotangent.reshape(tokens_dev, group_count, group_size, block).transpose(2, 0, 1, 3)
    heads_width = attention_probs.shape[1]
    outgoing = jnp.concatenate(
        [
            jnp.broadcast_to(attention_probs, (group_size,) + attention_probs.shape),
            by_position.reshape(group_size, tokens_dev, group_count * block),
        ],
        2,
    )
    incoming = lax.all_to_all(outgoing, GROUP, 0, 0, tiled=True)
    group_probs = incoming[:, :, :heads_width].reshape(group_size * tokens_dev, heads_width)
    group_cotangent = incoming[:, :, heads_width:].reshape(
        group_size * tokens_dev, group_count, block
    )
    weight_term = jnp.einsum(
        "th,tak->ahk", group_probs, group_cotangent, preferred_element_type=jnp.float32
    ) * (tokens_dev * n_ctx) ** (-0.5)
    weight_grad = lax.psum_scatter(weight_term, "cg", scatter_dimension=0, tiled=True)[0]
    grad_rows = attention_gradient.reshape(tokens_dev, kv_local, group_width, HEAD_SIZE)
    row_deltas = jnp.sum(grad_rows.astype(jnp.float32) * attn_rows.astype(jnp.float32), axis=-1)
    head_gradients = grad_rows.transpose(1, 0, 2, 3)
    delta_heads = row_deltas.transpose(1, 0, 2)
    query_parts, key_parts, value_parts = lax.map(
        lambda items: grad_band(
            items[0], items[1], items[2], items[3], items[4], items[5], full_mask
        ),
        (query_heads, head_gradients, log_totals, delta_heads, key_heads, value_heads),
    )
    key_ext_grad = key_parts.transpose(1, 0, 2).reshape(-1, kv_local * HEAD_SIZE)
    value_ext_grad = value_parts.transpose(1, 0, 2).reshape(-1, kv_local * HEAD_SIZE)
    pair_grad = jnp.concatenate([key_ext_grad, value_ext_grad], 1)
    pair_total = pair_grad[reach_count * tokens_dev :]
    for offset in range(1, reach_count + 1):
        first_row = (reach_count - offset) * tokens_dev
        sent = pair_grad[first_row : first_row + tokens_dev].astype(jnp.bfloat16)
        pair_total = pair_total + from_behind(sent, CTX, -offset).astype(jnp.float32)
    key_total = pair_total[:, :kv_width]
    value_total = pair_total[:, kv_width:]
    query_grad = query_parts.transpose(1, 0, 2, 3).reshape(tokens_dev, -1).astype(jnp.bfloat16)
    return (
        query_grad,
        key_total.astype(jnp.bfloat16),
        value_total.astype(jnp.bfloat16),
        weight_grad,
    )


GROUP_SIZE = 8
CTX = ("cg", "cz", "core")
GROUP = ("cz", "core")


def solution(mesh):
    n_ctx = mesh.shape["ctx"]
    devices = mesh.devices.reshape(n_ctx // GROUP_SIZE, GROUP_SIZE // 2, 2, mesh.shape["tp"])
    grouped = jax.sharding.Mesh(devices, ("cg", "cz", "core", "tp"))
    placed = (P(CTX, "tp"), P(CTX, "tp"), P(CTX, "tp"), P(CTX, "tp"), P("tp", CTX))
    return jax.shard_map(
        per_device,
        mesh=grouped,
        in_specs=placed,
        out_specs=(P(CTX, "tp"), P(CTX, "tp"), P(CTX, "tp"), P("tp", CTX)),
        check_vma=False,
    )
```

```python
import jax
import jax.numpy as jnp
from jax import lax
from jax.sharding import PartitionSpec as P

HEAD_SIZE = 128
WINDOW_SPAN = 1024
QUERY_HEAD_COUNT = 16
KEY_VALUE_HEADS = 8


score_scale = 168.0 ** (-0.5)


def from_behind(block, axis, distance):
    devices = range(lax.axis_size(axis))
    route = [(i - distance, i) for i in devices if i - distance in devices]
    return lax.ppermute(block, axis, route)


def band_mask(query_pos, key_pos):
    earlier = key_pos[None, :] <= query_pos[:, None]
    within = query_pos[:, None] - key_pos[None, :] < WINDOW_SPAN
    return earlier & within & (key_pos[None, :] >= 0)


def scores_for(query_head, key_head, allowed):
    scaled = (
        jnp.einsum("tgd,kd->gtk", query_head, key_head, preferred_element_type=jnp.float32)
        * score_scale
    )
    return jnp.where(allowed[None], scaled, -jnp.inf)


def forward_head(query_head, key_head, value_head, allowed):
    scores = scores_for(query_head, key_head, allowed)
    row_max = jnp.max(scores, axis=-1, keepdims=True)
    log_total = row_max + jnp.log(jnp.sum(jnp.exp(scores - row_max), axis=-1, keepdims=True))
    probs = jnp.exp(scores - log_total).astype(jnp.bfloat16)
    output = jnp.einsum("gtk,kd->tgd", probs, value_head, preferred_element_type=jnp.float32)
    return (output.astype(jnp.bfloat16), log_total[..., 0])


def grad_band(query_head, grad_head, log_total, delta_head, key_head, value_head, allowed):
    scores = scores_for(query_head, key_head, allowed)
    probs = jnp.exp(scores - log_total[..., None])
    probs_low = probs.astype(jnp.bfloat16)
    prob_grad = jnp.einsum("tgd,kd->gtk", grad_head, value_head, preferred_element_type=jnp.float32)
    score_grad = (probs * (prob_grad - delta_head.T[..., None])).astype(jnp.bfloat16)
    query_part = (
        jnp.einsum("gtk,kd->tgd", score_grad, key_head, preferred_element_type=jnp.float32)
        * score_scale
    )
    key_part = (
        jnp.einsum("gtk,tgd->kd", score_grad, query_head, preferred_element_type=jnp.float32)
        * score_scale
    )
    value_part = jnp.einsum("gtk,tgd->kd", probs_low, grad_head, preferred_element_type=jnp.float32)
    return (query_part, key_part, value_part)


def per_device(rotated_queries, rotated_keys, value_matrix, out_grad, out_weight):
    tokens_dev = rotated_queries.shape[0]
    n_ctx = lax.axis_size(("cg", "cp"))
    kv_local = rotated_keys.shape[1] // HEAD_SIZE
    group_width = QUERY_HEAD_COUNT // KEY_VALUE_HEADS
    reach_count = WINDOW_SPAN // tokens_dev
    start_pos = lax.axis_index(("cg", "cp")) * tokens_dev
    query_pos = start_pos + jnp.arange(tokens_dev, dtype=jnp.int32)
    kv_width = rotated_keys.shape[1]
    own_pair = jnp.concatenate([rotated_keys, value_matrix], 1)
    earlier = [from_behind(own_pair, ("cg", "cp"), offset) for offset in range(reach_count, 0, -1)]
    pair_ext = jnp.concatenate(earlier + [own_pair], 0)
    key_ext = pair_ext[:, :kv_width]
    value_ext = pair_ext[:, kv_width:]
    key_pos = (
        start_pos
        - reach_count * tokens_dev
        + jnp.arange((reach_count + 1) * tokens_dev, dtype=jnp.int32)
    )
    full_mask = band_mask(query_pos, key_pos)
    query_heads = rotated_queries.reshape(tokens_dev, kv_local, group_width, HEAD_SIZE).transpose(
        1, 0, 2, 3
    )
    key_heads = key_ext.reshape(-1, kv_local, HEAD_SIZE).transpose(1, 0, 2)
    value_heads = value_ext.reshape(-1, kv_local, HEAD_SIZE).transpose(1, 0, 2)
    attn_heads, log_totals = lax.map(
        lambda items: forward_head(items[0], items[1], items[2], full_mask),
        (query_heads, key_heads, value_heads),
    )
    attn_rows = attn_heads.transpose(1, 0, 2, 3)
    attention_probs = attn_rows.reshape(tokens_dev, -1)
    partner_grad = lax.ppermute(out_grad, "tp", [(0, 1), (1, 0)])
    cotangent = jnp.where(
        lax.axis_index("tp") == 0,
        jnp.concatenate([out_grad, partner_grad], 1),
        jnp.concatenate([partner_grad, out_grad], 1),
    )
    grad_sum = lax.dot_general(
        cotangent,
        lax.all_gather(out_weight, ("cg", "cp"), axis=1, tiled=True),
        (((1,), (1,)), ((), ())),
        preferred_element_type=jnp.float32,
    )
    attention_gradient = grad_sum.astype(jnp.bfloat16)
    group_size = lax.axis_size("cp")
    group_count = lax.axis_size("cg")
    block = cotangent.shape[1] // n_ctx
    by_position = cotangent.reshape(tokens_dev, group_count, group_size, block).transpose(2, 0, 1, 3)
    heads_width = attention_probs.shape[1]
    outgoing = jnp.concatenate(
        [
            jnp.broadcast_to(attention_probs, (group_size,) + attention_probs.shape),
            by_position.reshape(group_size, tokens_dev, group_count * block),
        ],
        2,
    )
    incoming = lax.all_to_all(outgoing, "cp", 0, 0, tiled=True)
    group_probs = incoming[:, :, :heads_width].reshape(group_size * tokens_dev, heads_width)
    group_cotangent = incoming[:, :, heads_width:].reshape(
        group_size * tokens_dev, group_count, block
    )
    weight_term = jnp.einsum(
        "th,tak->ahk", group_probs, group_cotangent, preferred_element_type=jnp.float32
    ) * (tokens_dev * n_ctx) ** (-0.5)
    weight_grad = jnp.sum(lax.all_to_all(weight_term, "cg", 0, 0, tiled=True), 0)
    grad_rows = attention_gradient.reshape(tokens_dev, kv_local, group_width, HEAD_SIZE)
    row_deltas = jnp.sum(grad_rows.astype(jnp.float32) * attn_rows.astype(jnp.float32), axis=-1)
    head_gradients = grad_rows.transpose(1, 0, 2, 3)
    delta_heads = row_deltas.transpose(1, 0, 2)
    query_parts, key_parts, value_parts = lax.map(
        lambda items: grad_band(
            items[0], items[1], items[2], items[3], items[4], items[5], full_mask
        ),
        (query_heads, head_gradients, log_totals, delta_heads, key_heads, value_heads),
    )
    key_ext_grad = key_parts.transpose(1, 0, 2).reshape(-1, kv_local * HEAD_SIZE)
    value_ext_grad = value_parts.transpose(1, 0, 2).reshape(-1, kv_local * HEAD_SIZE)
    pair_grad = jnp.concatenate([key_ext_grad, value_ext_grad], 1)
    pair_total = pair_grad[reach_count * tokens_dev :]
    for offset in range(1, reach_count + 1):
        first_row = (reach_count - offset) * tokens_dev
        sent = pair_grad[first_row : first_row + tokens_dev].astype(jnp.bfloat16)
        pair_total = pair_total + from_behind(sent, ("cg", "cp"), -offset).astype(jnp.float32)
    key_total = pair_total[:, :kv_width]
    value_total = pair_total[:, kv_width:]
    query_grad = query_parts.transpose(1, 0, 2, 3).reshape(tokens_dev, -1).astype(jnp.bfloat16)
    return (
        query_grad,
        key_total.astype(jnp.bfloat16),
        value_total.astype(jnp.bfloat16),
        weight_grad,
    )


GROUP_SIZE = 8


def solution(mesh):
    n_ctx = mesh.shape["ctx"]
    group_size = GROUP_SIZE if n_ctx % GROUP_SIZE == 0 else 1
    devices = mesh.devices.reshape(n_ctx // group_size, group_size, mesh.shape["tp"])
    grouped = jax.sharding.Mesh(devices, ("cg", "cp", "tp"))
    ctx = ("cg", "cp")
    placed = (P(ctx, "tp"), P(ctx, "tp"), P(ctx, "tp"), P(ctx, "tp"), P("tp", ctx))
    return jax.shard_map(
        per_device,
        mesh=grouped,
        in_specs=placed,
        out_specs=(P(ctx, "tp"), P(ctx, "tp"), P(ctx, "tp"), P("tp", ctx)),
        check_vma=False,
    )
```

```python
import jax
import jax.numpy as jnp
from jax import lax
from jax.sharding import PartitionSpec as P

HEAD_SIZE = 128
WINDOW_SPAN = 1024
QUERY_HEAD_COUNT = 16
KEY_VALUE_HEADS = 8


score_scale = 168.0 ** (-0.5)


def from_behind(block, axis, distance):
    devices = range(lax.axis_size(axis))
    route = [(i - distance, i) for i in devices if i - distance in devices]
    return lax.ppermute(block, axis, route)


def band_mask(query_pos, key_pos):
    earlier = key_pos[None, :] <= query_pos[:, None]
    within = query_pos[:, None] - key_pos[None, :] < WINDOW_SPAN
    return earlier & within & (key_pos[None, :] >= 0)


def scores_for(query_head, key_head, allowed):
    scaled = (
        jnp.einsum("tgd,kd->gtk", query_head, key_head, preferred_element_type=jnp.float32)
        * score_scale
    )
    return jnp.where(allowed[None], scaled, -jnp.inf)


def forward_head(query_head, key_head, value_head, allowed):
    scores = scores_for(query_head, key_head, allowed)
    row_max = jnp.max(scores, axis=-1, keepdims=True)
    log_total = row_max + jnp.log(jnp.sum(jnp.exp(scores - row_max), axis=-1, keepdims=True))
    probs = jnp.exp(scores - log_total).astype(jnp.bfloat16)
    output = jnp.einsum("gtk,kd->tgd", probs, value_head, preferred_element_type=jnp.float32)
    return (output.astype(jnp.bfloat16), log_total[..., 0])


def grad_band(query_head, grad_head, log_total, delta_head, key_head, value_head, allowed):
    scores = scores_for(query_head, key_head, allowed)
    probs = jnp.exp(scores - log_total[..., None])
    probs_low = probs.astype(jnp.bfloat16)
    prob_grad = jnp.einsum("tgd,kd->gtk", grad_head, value_head, preferred_element_type=jnp.float32)
    score_grad = (probs * (prob_grad - delta_head.T[..., None])).astype(jnp.bfloat16)
    query_part = (
        jnp.einsum("gtk,kd->tgd", score_grad, key_head, preferred_element_type=jnp.float32)
        * score_scale
    )
    key_part = (
        jnp.einsum("gtk,tgd->kd", score_grad, query_head, preferred_element_type=jnp.float32)
        * score_scale
    )
    value_part = jnp.einsum("gtk,tgd->kd", probs_low, grad_head, preferred_element_type=jnp.float32)
    return (query_part, key_part, value_part)


def per_device(rotated_queries, rotated_keys, value_matrix, out_grad, out_weight):
    tokens_dev = rotated_queries.shape[0]
    n_ctx = lax.axis_size(("cg", "cp"))
    kv_local = rotated_keys.shape[1] // HEAD_SIZE
    group_width = QUERY_HEAD_COUNT // KEY_VALUE_HEADS
    reach_count = WINDOW_SPAN // tokens_dev
    start_pos = lax.axis_index(("cg", "cp")) * tokens_dev
    query_pos = start_pos + jnp.arange(tokens_dev, dtype=jnp.int32)
    kv_width = rotated_keys.shape[1]
    own_pair = jnp.concatenate([rotated_keys, value_matrix], 1)
    earlier = [from_behind(own_pair, ("cg", "cp"), offset) for offset in range(reach_count, 0, -1)]
    pair_ext = jnp.concatenate(earlier + [own_pair], 0)
    key_ext = pair_ext[:, :kv_width]
    value_ext = pair_ext[:, kv_width:]
    key_pos = (
        start_pos
        - reach_count * tokens_dev
        + jnp.arange((reach_count + 1) * tokens_dev, dtype=jnp.int32)
    )
    full_mask = band_mask(query_pos, key_pos)
    query_heads = rotated_queries.reshape(tokens_dev, kv_local, group_width, HEAD_SIZE).transpose(
        1, 0, 2, 3
    )
    key_heads = key_ext.reshape(-1, kv_local, HEAD_SIZE).transpose(1, 0, 2)
    value_heads = value_ext.reshape(-1, kv_local, HEAD_SIZE).transpose(1, 0, 2)
    attn_heads, log_totals = lax.map(
        lambda items: forward_head(items[0], items[1], items[2], full_mask),
        (query_heads, key_heads, value_heads),
    )
    attn_rows = attn_heads.transpose(1, 0, 2, 3)
    attention_probs = attn_rows.reshape(tokens_dev, -1)
    partner_grad = lax.ppermute(out_grad, "tp", [(0, 1), (1, 0)])
    cotangent = jnp.where(
        lax.axis_index("tp") == 0,
        jnp.concatenate([out_grad, partner_grad], 1),
        jnp.concatenate([partner_grad, out_grad], 1),
    )
    group_size = lax.axis_size("cp")
    group_count = lax.axis_size("cg")
    block = cotangent.shape[1] // n_ctx
    weight_rows = out_weight.T
    group_weights = lax.all_to_all(
        jnp.broadcast_to(weight_rows, (group_size,) + weight_rows.shape), "cp", 0, 0, tiled=True
    ).reshape(group_size * block, -1)
    by_group = cotangent.reshape(tokens_dev, group_count, group_size * block).transpose(1, 0, 2)
    group_columns = lax.all_to_all(by_group, "cg", 0, 0, tiled=True)
    partial_grads = jnp.einsum(
        "btk,kh->bth", group_columns, group_weights, preferred_element_type=jnp.float32
    )
    grad_sum = jnp.sum(lax.all_to_all(partial_grads, "cg", 0, 0, tiled=True), 0)
    by_position = cotangent.reshape(tokens_dev, group_count, group_size, block).transpose(2, 0, 1, 3)
    heads_width = attention_probs.shape[1]
    outgoing = jnp.concatenate(
        [
            jnp.broadcast_to(attention_probs, (group_size,) + attention_probs.shape),
            by_position.reshape(group_size, tokens_dev, group_count * block),
        ],
        2,
    )
    outgoing, grad_sum = lax.optimization_barrier((outgoing, grad_sum))
    attention_gradient = grad_sum.astype(jnp.bfloat16)
    incoming = lax.all_to_all(outgoing, "cp", 0, 0, tiled=True)
    group_probs = incoming[:, :, :heads_width].reshape(group_size * tokens_dev, heads_width)
    group_cotangent = incoming[:, :, heads_width:].reshape(
        group_size * tokens_dev, group_count, block
    )
    weight_term = jnp.einsum(
        "th,tak->ahk", group_probs, group_cotangent, preferred_element_type=jnp.float32
    ) * (tokens_dev * n_ctx) ** (-0.5)
    grad_rows = attention_gradient.reshape(tokens_dev, kv_local, group_width, HEAD_SIZE)
    row_deltas = jnp.sum(grad_rows.astype(jnp.float32) * attn_rows.astype(jnp.float32), axis=-1)
    head_gradients = grad_rows.transpose(1, 0, 2, 3)
    delta_heads = row_deltas.transpose(1, 0, 2)
    query_parts, key_parts, value_parts = lax.map(
        lambda items: grad_band(
            items[0], items[1], items[2], items[3], items[4], items[5], full_mask
        ),
        (query_heads, head_gradients, log_totals, delta_heads, key_heads, value_heads),
    )
    weight_term, query_parts, key_parts, value_parts = lax.optimization_barrier(
        (weight_term, query_parts, key_parts, value_parts)
    )
    weight_grad = jnp.sum(lax.all_to_all(weight_term, "cg", 0, 0, tiled=True), 0)
    key_ext_grad = key_parts.transpose(1, 0, 2).reshape(-1, kv_local * HEAD_SIZE)
    value_ext_grad = value_parts.transpose(1, 0, 2).reshape(-1, kv_local * HEAD_SIZE)
    pair_grad = jnp.concatenate([key_ext_grad, value_ext_grad], 1)
    pair_total = pair_grad[reach_count * tokens_dev :]
    for offset in range(1, reach_count + 1):
        first_row = (reach_count - offset) * tokens_dev
        sent = pair_grad[first_row : first_row + tokens_dev].astype(jnp.bfloat16)
        pair_total = pair_total + from_behind(sent, ("cg", "cp"), -offset).astype(jnp.float32)
    key_total = pair_total[:, :kv_width]
    value_total = pair_total[:, kv_width:]
    query_grad = query_parts.transpose(1, 0, 2, 3).reshape(tokens_dev, -1).astype(jnp.bfloat16)
    return (
        query_grad,
        key_total.astype(jnp.bfloat16),
        value_total.astype(jnp.bfloat16),
        weight_grad,
    )


GROUP_SIZE = 8


def solution(mesh):
    n_ctx = mesh.shape["ctx"]
    group_size = GROUP_SIZE if n_ctx % GROUP_SIZE == 0 else 1
    devices = mesh.devices.reshape(n_ctx // group_size, group_size, mesh.shape["tp"])
    grouped = jax.sharding.Mesh(devices, ("cg", "cp", "tp"))
    ctx = ("cg", "cp")
    placed = (P(ctx, "tp"), P(ctx, "tp"), P(ctx, "tp"), P(ctx, "tp"), P("tp", ctx))
    return jax.shard_map(
        per_device,
        mesh=grouped,
        in_specs=placed,
        out_specs=(P(ctx, "tp"), P(ctx, "tp"), P(ctx, "tp"), P("tp", ctx)),
        check_vma=False,
    )
```

```python
import jax
import jax.numpy as jnp
from jax import lax
from jax.sharding import PartitionSpec as P

HEAD_SIZE = 128
WINDOW_SPAN = 1024
QUERY_HEAD_COUNT = 16
KEY_VALUE_HEADS = 8


score_scale = 168.0 ** (-0.5)


def from_behind(block, axis, distance):
    devices = range(lax.axis_size(axis))
    route = [(i - distance, i) for i in devices if i - distance in devices]
    return lax.ppermute(block, axis, route)


def band_mask(query_pos, key_pos):
    earlier = key_pos[None, :] <= query_pos[:, None]
    within = query_pos[:, None] - key_pos[None, :] < WINDOW_SPAN
    return earlier & within & (key_pos[None, :] >= 0)


def scores_for(query_head, key_head, allowed):
    scaled = (
        jnp.einsum("tgd,kd->gtk", query_head, key_head, preferred_element_type=jnp.float32)
        * score_scale
    )
    return jnp.where(allowed[None], scaled, -jnp.inf)


def forward_head(query_head, key_head, value_head, allowed):
    scores = scores_for(query_head, key_head, allowed)
    row_max = jnp.max(scores, axis=-1, keepdims=True)
    log_total = row_max + jnp.log(jnp.sum(jnp.exp(scores - row_max), axis=-1, keepdims=True))
    probs = jnp.exp(scores - log_total).astype(jnp.bfloat16)
    output = jnp.einsum("gtk,kd->tgd", probs, value_head, preferred_element_type=jnp.float32)
    return (output.astype(jnp.bfloat16), log_total[..., 0])


def grad_band(query_head, grad_head, log_total, delta_head, key_head, value_head, allowed):
    scores = scores_for(query_head, key_head, allowed)
    probs = jnp.exp(scores - log_total[..., None])
    probs_low = probs.astype(jnp.bfloat16)
    prob_grad = jnp.einsum("tgd,kd->gtk", grad_head, value_head, preferred_element_type=jnp.float32)
    score_grad = (probs * (prob_grad - delta_head.T[..., None])).astype(jnp.bfloat16)
    query_part = (
        jnp.einsum("gtk,kd->tgd", score_grad, key_head, preferred_element_type=jnp.float32)
        * score_scale
    )
    key_part = (
        jnp.einsum("gtk,tgd->kd", score_grad, query_head, preferred_element_type=jnp.float32)
        * score_scale
    )
    value_part = jnp.einsum("gtk,tgd->kd", probs_low, grad_head, preferred_element_type=jnp.float32)
    return (query_part, key_part, value_part)


def per_device(rotated_queries, rotated_keys, value_matrix, out_grad, out_weight):
    tokens_dev = rotated_queries.shape[0]
    n_ctx = lax.axis_size(("cg", "cp"))
    kv_local = rotated_keys.shape[1] // HEAD_SIZE
    group_width = QUERY_HEAD_COUNT // KEY_VALUE_HEADS
    reach_count = WINDOW_SPAN // tokens_dev
    start_pos = lax.axis_index(("cg", "cp")) * tokens_dev
    query_pos = start_pos + jnp.arange(tokens_dev, dtype=jnp.int32)
    kv_width = rotated_keys.shape[1]
    own_pair = jnp.concatenate([rotated_keys, value_matrix], 1)
    earlier = [from_behind(own_pair, ("cg", "cp"), offset) for offset in range(reach_count, 0, -1)]
    pair_ext = jnp.concatenate(earlier + [own_pair], 0)
    key_ext = pair_ext[:, :kv_width]
    value_ext = pair_ext[:, kv_width:]
    key_pos = (
        start_pos
        - reach_count * tokens_dev
        + jnp.arange((reach_count + 1) * tokens_dev, dtype=jnp.int32)
    )
    full_mask = band_mask(query_pos, key_pos)
    query_heads = rotated_queries.reshape(tokens_dev, kv_local, group_width, HEAD_SIZE).transpose(
        1, 0, 2, 3
    )
    key_heads = key_ext.reshape(-1, kv_local, HEAD_SIZE).transpose(1, 0, 2)
    value_heads = value_ext.reshape(-1, kv_local, HEAD_SIZE).transpose(1, 0, 2)
    attn_heads, log_totals = lax.map(
        lambda items: forward_head(items[0], items[1], items[2], full_mask),
        (query_heads, key_heads, value_heads),
    )
    attn_rows = attn_heads.transpose(1, 0, 2, 3)
    attention_probs = attn_rows.reshape(tokens_dev, -1)
    partner_grad = lax.ppermute(out_grad, "tp", [(0, 1), (1, 0)])
    cotangent = jnp.where(
        lax.axis_index("tp") == 0,
        jnp.concatenate([out_grad, partner_grad], 1),
        jnp.concatenate([partner_grad, out_grad], 1),
    )
    group_size = lax.axis_size("cp")
    group_count = lax.axis_size("cg")
    block = cotangent.shape[1] // n_ctx
    weight_rows = out_weight.T
    group_weights = lax.all_to_all(
        jnp.broadcast_to(weight_rows, (group_size,) + weight_rows.shape), "cp", 0, 0, tiled=True
    ).reshape(group_size * block, -1)
    by_group = cotangent.reshape(tokens_dev, group_count, group_size * block).transpose(1, 0, 2)
    group_columns = lax.all_to_all(by_group, "cg", 0, 0, tiled=True)
    partial_grads = jnp.einsum(
        "btk,kh->bth", group_columns, group_weights, preferred_element_type=jnp.float32
    )
    grad_sum = jnp.sum(
        lax.all_to_all(partial_grads.astype(jnp.bfloat16), "cg", 0, 0, tiled=True).astype(
            jnp.float32
        ),
        0,
    )
    by_position = cotangent.reshape(tokens_dev, group_count, group_size, block).transpose(2, 0, 1, 3)
    heads_width = attention_probs.shape[1]
    outgoing = jnp.concatenate(
        [
            jnp.broadcast_to(attention_probs, (group_size,) + attention_probs.shape),
            by_position.reshape(group_size, tokens_dev, group_count * block),
        ],
        2,
    )
    outgoing, grad_sum = lax.optimization_barrier((outgoing, grad_sum))
    attention_gradient = grad_sum.astype(jnp.bfloat16)
    incoming = lax.all_to_all(outgoing, "cp", 0, 0, tiled=True)
    group_probs = incoming[:, :, :heads_width].reshape(group_size * tokens_dev, heads_width)
    group_cotangent = incoming[:, :, heads_width:].reshape(
        group_size * tokens_dev, group_count, block
    )
    grad_rows = attention_gradient.reshape(tokens_dev, kv_local, group_width, HEAD_SIZE)
    row_deltas = jnp.sum(grad_rows.astype(jnp.float32) * attn_rows.astype(jnp.float32), axis=-1)
    head_gradients = grad_rows.transpose(1, 0, 2, 3)
    delta_heads = row_deltas.transpose(1, 0, 2)
    query_parts, key_parts, value_parts = lax.map(
        lambda items: grad_band(
            items[0], items[1], items[2], items[3], items[4], items[5], full_mask
        ),
        (query_heads, head_gradients, log_totals, delta_heads, key_heads, value_heads),
    )
    key_ext_grad = key_parts.transpose(1, 0, 2).reshape(-1, kv_local * HEAD_SIZE)
    value_ext_grad = value_parts.transpose(1, 0, 2).reshape(-1, kv_local * HEAD_SIZE)
    pair_grad = jnp.concatenate([key_ext_grad, value_ext_grad], 1)
    pair_total = pair_grad[reach_count * tokens_dev :]
    sent = [
        pair_grad[(reach_count - offset) * tokens_dev : (reach_count - offset + 1) * tokens_dev]
        for offset in range(1, reach_count + 1)
    ]
    sent = [block.astype(jnp.bfloat16) for block in sent]
    for offset in range(1, reach_count + 1):
        arrived = from_behind(sent[offset - 1], ("cg", "cp"), -offset)
        pair_total = pair_total + arrived.astype(jnp.float32)
    group_probs, group_cotangent, sent = lax.optimization_barrier(
        (group_probs, group_cotangent, sent)
    )
    weight_term = jnp.einsum(
        "th,tak->ahk", group_probs, group_cotangent, preferred_element_type=jnp.float32
    ) * (tokens_dev * n_ctx) ** (-0.5)
    weight_grad = jnp.sum(lax.all_to_all(weight_term, "cg", 0, 0, tiled=True), 0)
    key_total = pair_total[:, :kv_width]
    value_total = pair_total[:, kv_width:]
    query_grad = query_parts.transpose(1, 0, 2, 3).reshape(tokens_dev, -1).astype(jnp.bfloat16)
    return (
        query_grad,
        key_total.astype(jnp.bfloat16),
        value_total.astype(jnp.bfloat16),
        weight_grad,
    )


GROUP_SIZE = 8


def solution(mesh):
    n_ctx = mesh.shape["ctx"]
    group_size = GROUP_SIZE if n_ctx % GROUP_SIZE == 0 else 1
    devices = mesh.devices.reshape(n_ctx // group_size, group_size, mesh.shape["tp"])
    grouped = jax.sharding.Mesh(devices, ("cg", "cp", "tp"))
    ctx = ("cg", "cp")
    placed = (P(ctx, "tp"), P(ctx, "tp"), P(ctx, "tp"), P(ctx, "tp"), P("tp", ctx))
    return jax.shard_map(
        per_device,
        mesh=grouped,
        in_specs=placed,
        out_specs=(P(ctx, "tp"), P(ctx, "tp"), P(ctx, "tp"), P("tp", ctx)),
        check_vma=False,
    )
```

```python
import jax
import jax.numpy as jnp
from jax import lax
from jax.sharding import PartitionSpec as P


HEAD_SIZE = 128
WINDOW_SPAN = 1024
QUERY_HEAD_COUNT = 16
KEY_VALUE_HEADS = 8


score_scale = 168.0 ** (-0.5)


def from_behind(block, axis, distance):
    devices = range(lax.axis_size(axis))
    route = [(i - distance, i) for i in devices if i - distance in devices]
    return lax.ppermute(block, axis, route)


def band_mask(query_pos, key_pos):
    earlier = key_pos[None, :] <= query_pos[:, None]
    within = query_pos[:, None] - key_pos[None, :] < WINDOW_SPAN
    return earlier & within & (key_pos[None, :] >= 0)


def scores_for(query_head, key_head, allowed):
    scaled = (
        jnp.einsum("tgd,kd->gtk", query_head, key_head, preferred_element_type=jnp.float32)
        * score_scale
    )
    return jnp.where(allowed[None], scaled, -jnp.inf)


def forward_head(query_head, key_head, value_head, allowed):
    scores = scores_for(query_head, key_head, allowed)
    row_max = jnp.max(scores, axis=-1, keepdims=True)
    log_total = row_max + jnp.log(jnp.sum(jnp.exp(scores - row_max), axis=-1, keepdims=True))
    probs = jnp.exp(scores - log_total).astype(jnp.bfloat16)
    output = jnp.einsum("gtk,kd->tgd", probs, value_head, preferred_element_type=jnp.float32)
    return (output.astype(jnp.bfloat16), log_total[..., 0])


def grad_band(query_head, grad_head, log_total, delta_head, key_head, value_head, allowed):
    scores = scores_for(query_head, key_head, allowed)
    probs = jnp.exp(scores - log_total[..., None])
    probs_low = probs.astype(jnp.bfloat16)
    prob_grad = jnp.einsum("tgd,kd->gtk", grad_head, value_head, preferred_element_type=jnp.float32)
    score_grad = (probs * (prob_grad - delta_head.T[..., None])).astype(jnp.bfloat16)
    query_part = (
        jnp.einsum("gtk,kd->tgd", score_grad, key_head, preferred_element_type=jnp.float32)
        * score_scale
    )
    key_part = (
        jnp.einsum("gtk,tgd->kd", score_grad, query_head, preferred_element_type=jnp.float32)
        * score_scale
    )
    value_part = jnp.einsum("gtk,tgd->kd", probs_low, grad_head, preferred_element_type=jnp.float32)
    return (query_part, key_part, value_part)


def device_body(rotated_queries, rotated_keys, value_matrix, out_grad, out_weight):
    tokens_dev = rotated_queries.shape[0]
    n_ctx = lax.axis_size(("cg", "cp"))
    kv_local = rotated_keys.shape[1] // HEAD_SIZE
    group_width = QUERY_HEAD_COUNT // KEY_VALUE_HEADS
    reach_count = WINDOW_SPAN // tokens_dev
    start_pos = lax.axis_index(("cg", "cp")) * tokens_dev
    query_pos = start_pos + jnp.arange(tokens_dev, dtype=jnp.int32)
    kv_width = rotated_keys.shape[1]
    own_pair = jnp.concatenate([rotated_keys, value_matrix], 1)
    earlier = [from_behind(own_pair, ("cg", "cp"), offset) for offset in range(reach_count, 0, -1)]
    pair_ext = jnp.concatenate(earlier + [own_pair], 0)
    key_ext = pair_ext[:, :kv_width]
    value_ext = pair_ext[:, kv_width:]
    key_pos = (
        start_pos
        - reach_count * tokens_dev
        + jnp.arange((reach_count + 1) * tokens_dev, dtype=jnp.int32)
    )
    full_mask = band_mask(query_pos, key_pos)
    query_heads = rotated_queries.reshape(tokens_dev, kv_local, group_width, HEAD_SIZE).transpose(
        1, 0, 2, 3
    )
    key_heads = key_ext.reshape(-1, kv_local, HEAD_SIZE).transpose(1, 0, 2)
    value_heads = value_ext.reshape(-1, kv_local, HEAD_SIZE).transpose(1, 0, 2)
    attn_heads, log_totals = lax.map(
        lambda items: forward_head(items[0], items[1], items[2], full_mask),
        (query_heads, key_heads, value_heads),
    )
    attn_rows = attn_heads.transpose(1, 0, 2, 3)
    attention_probs = attn_rows.reshape(tokens_dev, -1)
    partner_grad = lax.ppermute(out_grad, "tp", [(0, 1), (1, 0)])
    cotangent = jnp.where(
        lax.axis_index("tp") == 0,
        jnp.concatenate([out_grad, partner_grad], 1),
        jnp.concatenate([partner_grad, out_grad], 1),
    )
    group_size = lax.axis_size("cp")
    group_count = lax.axis_size("cg")
    block = cotangent.shape[1] // n_ctx
    weight_rows = out_weight.T
    by_position = cotangent.reshape(tokens_dev, group_count, group_size, block).transpose(2, 0, 1, 3)
    lanes = 128
    weight_flat = weight_rows.reshape(-1, lanes)
    packed = jnp.concatenate(
        [
            jnp.broadcast_to(weight_flat, (group_size,) + weight_flat.shape),
            by_position.reshape(group_size, -1, lanes),
        ],
        1,
    )
    unpacked = lax.all_to_all(packed, "cp", 0, 0, tiled=True)
    weight_count = weight_flat.shape[0]
    group_weights = unpacked[:, :weight_count].reshape(group_size * block, -1)
    group_cotangent = unpacked[:, weight_count:].reshape(
        group_size * tokens_dev, group_count, block
    )
    by_group = cotangent.reshape(tokens_dev, group_count, group_size * block).transpose(1, 0, 2)
    group_columns = lax.all_to_all(by_group, "cg", 0, 0, tiled=True)
    partial_grads = jnp.einsum(
        "btk,kh->bth", group_columns, group_weights, preferred_element_type=jnp.float32
    )
    grad_sum = jnp.sum(
        lax.all_to_all(partial_grads.astype(jnp.bfloat16), "cg", 0, 0, tiled=True).astype(
            jnp.float32
        ),
        0,
    )
    attention_gradient = grad_sum.astype(jnp.bfloat16)
    group_probs = lax.all_gather(attention_probs, "cp", axis=0, tiled=True)
    grad_rows = attention_gradient.reshape(tokens_dev, kv_local, group_width, HEAD_SIZE)
    row_deltas = jnp.sum(grad_rows.astype(jnp.float32) * attn_rows.astype(jnp.float32), axis=-1)
    head_gradients = grad_rows.transpose(1, 0, 2, 3)
    delta_heads = row_deltas.transpose(1, 0, 2)
    query_parts, key_parts, value_parts = lax.map(
        lambda items: grad_band(
            items[0], items[1], items[2], items[3], items[4], items[5], full_mask
        ),
        (query_heads, head_gradients, log_totals, delta_heads, key_heads, value_heads),
    )
    key_ext_grad = key_parts.transpose(1, 0, 2).reshape(-1, kv_local * HEAD_SIZE)
    value_ext_grad = value_parts.transpose(1, 0, 2).reshape(-1, kv_local * HEAD_SIZE)
    pair_grad = jnp.concatenate([key_ext_grad, value_ext_grad], 1)
    pair_total = pair_grad[reach_count * tokens_dev :]
    sent = [
        pair_grad[(reach_count - offset) * tokens_dev : (reach_count - offset + 1) * tokens_dev]
        for offset in range(1, reach_count + 1)
    ]
    sent = [block.astype(jnp.bfloat16) for block in sent]
    for offset in range(1, reach_count + 1):
        arrived = from_behind(sent[offset - 1], ("cg", "cp"), -offset)
        pair_total = pair_total + arrived.astype(jnp.float32)
    group_probs, group_cotangent, sent = lax.optimization_barrier(
        (group_probs, group_cotangent, sent)
    )
    weight_term = jnp.einsum(
        "th,tak->ahk", group_probs, group_cotangent, preferred_element_type=jnp.float32
    ) * (tokens_dev * n_ctx) ** (-0.5)
    weight_grad = jnp.sum(lax.all_to_all(weight_term, "cg", 0, 0, tiled=True), 0)
    key_total = pair_total[:, :kv_width]
    value_total = pair_total[:, kv_width:]
    query_grad = query_parts.transpose(1, 0, 2, 3).reshape(tokens_dev, -1).astype(jnp.bfloat16)
    return (
        query_grad,
        key_total.astype(jnp.bfloat16),
        value_total.astype(jnp.bfloat16),
        weight_grad,
    )


GROUP_SIZE = 8


def solution(mesh):
    n_ctx = mesh.shape["ctx"]
    group_size = GROUP_SIZE if n_ctx % GROUP_SIZE == 0 else 1
    devices = mesh.devices.reshape(n_ctx // group_size, group_size, mesh.shape["tp"])
    grouped = jax.sharding.Mesh(devices, ("cg", "cp", "tp"))
    ctx = ("cg", "cp")
    placed = (P(ctx, "tp"), P(ctx, "tp"), P(ctx, "tp"), P(ctx, "tp"), P("tp", ctx))
    return jax.shard_map(
        device_body,
        mesh=grouped,
        in_specs=placed,
        out_specs=(P(ctx, "tp"), P(ctx, "tp"), P(ctx, "tp"), P("tp", ctx)),
        check_vma=False,
    )
```

```python
import jax
import jax.numpy as jnp
from jax import lax
from jax.sharding import PartitionSpec as P


HEAD_SIZE = 128
WINDOW_SPAN = 1024
QUERY_HEAD_COUNT = 16
KEY_VALUE_HEADS = 8


score_scale = 168.0 ** (-0.5)


def from_behind(block, axis, distance):
    devices = range(lax.axis_size(axis))
    route = [(i - distance, i) for i in devices if i - distance in devices]
    return lax.ppermute(block, axis, route)


def band_mask(query_pos, key_pos):
    earlier = key_pos[None, :] <= query_pos[:, None]
    within = query_pos[:, None] - key_pos[None, :] < WINDOW_SPAN
    return earlier & within & (key_pos[None, :] >= 0)


def scores_for(query_head, key_head, allowed):
    scaled = (
        jnp.einsum("tgd,kd->gtk", query_head, key_head, preferred_element_type=jnp.float32)
        * score_scale
    )
    return jnp.where(allowed[None], scaled, -jnp.inf)


def forward_head(query_head, key_head, value_head, allowed):
    scores = scores_for(query_head, key_head, allowed)
    row_max = jnp.max(scores, axis=-1, keepdims=True)
    log_total = row_max + jnp.log(jnp.sum(jnp.exp(scores - row_max), axis=-1, keepdims=True))
    probs = jnp.exp(scores - log_total).astype(jnp.bfloat16)
    output = jnp.einsum("gtk,kd->tgd", probs, value_head, preferred_element_type=jnp.float32)
    return (output.astype(jnp.bfloat16), log_total[..., 0])


def grad_band(query_head, grad_head, log_total, delta_head, key_head, value_head, allowed):
    scores = scores_for(query_head, key_head, allowed)
    probs = jnp.exp(scores - log_total[..., None])
    probs_low = probs.astype(jnp.bfloat16)
    prob_grad = jnp.einsum("tgd,kd->gtk", grad_head, value_head, preferred_element_type=jnp.float32)
    score_grad = (probs * (prob_grad - delta_head.T[..., None])).astype(jnp.bfloat16)
    query_part = (
        jnp.einsum("gtk,kd->tgd", score_grad, key_head, preferred_element_type=jnp.float32)
        * score_scale
    )
    key_part = (
        jnp.einsum("gtk,tgd->kd", score_grad, query_head, preferred_element_type=jnp.float32)
        * score_scale
    )
    value_part = jnp.einsum("gtk,tgd->kd", probs_low, grad_head, preferred_element_type=jnp.float32)
    return (query_part, key_part, value_part)


def device_body(rotated_queries, rotated_keys, value_matrix, out_grad, out_weight):
    tokens_dev = rotated_queries.shape[0]
    n_ctx = lax.axis_size(("cg", "cp"))
    kv_local = rotated_keys.shape[1] // HEAD_SIZE
    group_width = QUERY_HEAD_COUNT // KEY_VALUE_HEADS
    reach_count = WINDOW_SPAN // tokens_dev
    start_pos = lax.axis_index(("cg", "cp")) * tokens_dev
    query_pos = start_pos + jnp.arange(tokens_dev, dtype=jnp.int32)
    kv_width = rotated_keys.shape[1]
    own_pair = jnp.concatenate([rotated_keys, value_matrix], 1)
    earlier = [from_behind(own_pair, ("cg", "cp"), offset) for offset in range(reach_count, 0, -1)]
    pair_ext = jnp.concatenate(earlier + [own_pair], 0)
    key_ext = pair_ext[:, :kv_width]
    value_ext = pair_ext[:, kv_width:]
    key_pos = (
        start_pos
        - reach_count * tokens_dev
        + jnp.arange((reach_count + 1) * tokens_dev, dtype=jnp.int32)
    )
    full_mask = band_mask(query_pos, key_pos)
    query_heads = rotated_queries.reshape(tokens_dev, kv_local, group_width, HEAD_SIZE).transpose(
        1, 0, 2, 3
    )
    key_heads = key_ext.reshape(-1, kv_local, HEAD_SIZE).transpose(1, 0, 2)
    value_heads = value_ext.reshape(-1, kv_local, HEAD_SIZE).transpose(1, 0, 2)
    attn_heads, log_totals = lax.map(
        lambda items: forward_head(items[0], items[1], items[2], full_mask),
        (query_heads, key_heads, value_heads),
    )
    attn_rows = attn_heads.transpose(1, 0, 2, 3)
    attention_probs = attn_rows.reshape(tokens_dev, -1)
    partner_grad = lax.ppermute(out_grad, "tp", [(0, 1), (1, 0)])
    cotangent = jnp.where(
        lax.axis_index("tp") == 0,
        jnp.concatenate([out_grad, partner_grad], 1),
        jnp.concatenate([partner_grad, out_grad], 1),
    )
    group_size = lax.axis_size("cp")
    group_count = lax.axis_size("cg")
    block = cotangent.shape[1] // n_ctx
    weight_rows = out_weight.T
    group_weights = lax.all_to_all(
        jnp.broadcast_to(weight_rows, (group_count,) + weight_rows.shape), "cg", 0, 0, tiled=True
    ).reshape(group_count * block, -1)
    by_group = (
        cotangent.reshape(tokens_dev, group_count, group_size, block)
        .transpose(2, 0, 1, 3)
        .reshape(group_size, tokens_dev, group_count * block)
    )
    group_columns = lax.all_to_all(by_group, "cp", 0, 0, tiled=True)
    partial_grads = jnp.einsum(
        "btk,kh->bth", group_columns, group_weights, preferred_element_type=jnp.float32
    )
    grad_sum = jnp.sum(
        lax.all_to_all(partial_grads.astype(jnp.bfloat16), "cp", 0, 0, tiled=True).astype(
            jnp.float32
        ),
        0,
    )
    attention_gradient = grad_sum.astype(jnp.bfloat16)
    group_probs = lax.all_gather(attention_probs, "cp", axis=0, tiled=True)
    grad_rows = attention_gradient.reshape(tokens_dev, kv_local, group_width, HEAD_SIZE)
    row_deltas = jnp.sum(grad_rows.astype(jnp.float32) * attn_rows.astype(jnp.float32), axis=-1)
    head_gradients = grad_rows.transpose(1, 0, 2, 3)
    delta_heads = row_deltas.transpose(1, 0, 2)
    query_parts, key_parts, value_parts = lax.map(
        lambda items: grad_band(
            items[0], items[1], items[2], items[3], items[4], items[5], full_mask
        ),
        (query_heads, head_gradients, log_totals, delta_heads, key_heads, value_heads),
    )
    key_ext_grad = key_parts.transpose(1, 0, 2).reshape(-1, kv_local * HEAD_SIZE)
    value_ext_grad = value_parts.transpose(1, 0, 2).reshape(-1, kv_local * HEAD_SIZE)
    pair_grad = jnp.concatenate([key_ext_grad, value_ext_grad], 1)
    pair_total = pair_grad[reach_count * tokens_dev :]
    sent = [
        pair_grad[(reach_count - offset) * tokens_dev : (reach_count - offset + 1) * tokens_dev]
        for offset in range(1, reach_count + 1)
    ]
    sent = [block.astype(jnp.bfloat16) for block in sent]
    for offset in range(1, reach_count + 1):
        arrived = from_behind(sent[offset - 1], ("cg", "cp"), -offset)
        pair_total = pair_total + arrived.astype(jnp.float32)
    group_probs, group_columns, sent = lax.optimization_barrier((group_probs, group_columns, sent))
    weight_term = jnp.einsum(
        "th,tqk->qhk",
        group_probs,
        group_columns.reshape(group_size * tokens_dev, group_count, block),
        preferred_element_type=jnp.float32,
    ) * (tokens_dev * n_ctx) ** (-0.5)
    weight_parts = lax.all_to_all(weight_term.astype(jnp.bfloat16), "cg", 0, 0, tiled=True)
    weight_grad = jnp.sum(weight_parts.astype(jnp.float32), 0)
    key_total = pair_total[:, :kv_width]
    value_total = pair_total[:, kv_width:]
    query_grad = query_parts.transpose(1, 0, 2, 3).reshape(tokens_dev, -1).astype(jnp.bfloat16)
    return (
        query_grad,
        key_total.astype(jnp.bfloat16),
        value_total.astype(jnp.bfloat16),
        weight_grad,
    )


GROUP_SIZE = 8


def solution(mesh):
    n_ctx = mesh.shape["ctx"]
    group_size = GROUP_SIZE if n_ctx % GROUP_SIZE == 0 else 1
    devices = mesh.devices.reshape(n_ctx // group_size, group_size, mesh.shape["tp"])
    grouped = jax.sharding.Mesh(devices, ("cg", "cp", "tp"))
    ctx = ("cg", "cp")
    placed = (P(ctx, "tp"), P(ctx, "tp"), P(ctx, "tp"), P(ctx, "tp"), P("tp", ctx))
    return jax.shard_map(
        device_body,
        mesh=grouped,
        in_specs=placed,
        out_specs=(P(ctx, "tp"), P(ctx, "tp"), P(ctx, "tp"), P("tp", ctx)),
        check_vma=False,
    )
```

```python
import jax
import jax.numpy as jnp
from jax import lax
from jax.sharding import PartitionSpec as P


HEAD_SIZE = 128
WINDOW_SPAN = 1024
QUERY_HEAD_COUNT = 16
KEY_VALUE_HEADS = 8


score_scale = 168.0 ** (-0.5)


def from_behind(block, axis, distance):
    devices = range(lax.axis_size(axis))
    route = [(i - distance, i) for i in devices if i - distance in devices]
    return lax.ppermute(block, axis, route)


def band_mask(query_pos, key_pos):
    earlier = key_pos[None, :] <= query_pos[:, None]
    within = query_pos[:, None] - key_pos[None, :] < WINDOW_SPAN
    return earlier & within & (key_pos[None, :] >= 0)


def scores_for(query_head, key_head, allowed):
    scaled = (
        jnp.einsum("tgd,kd->gtk", query_head, key_head, preferred_element_type=jnp.float32)
        * score_scale
    )
    return jnp.where(allowed[None], scaled, -jnp.inf)


def forward_head(query_head, key_head, value_head, allowed):
    scores = scores_for(query_head, key_head, allowed)
    row_max = jnp.max(scores, axis=-1, keepdims=True)
    log_total = row_max + jnp.log(jnp.sum(jnp.exp(scores - row_max), axis=-1, keepdims=True))
    probs = jnp.exp(scores - log_total).astype(jnp.bfloat16)
    output = jnp.einsum("gtk,kd->tgd", probs, value_head, preferred_element_type=jnp.float32)
    return (output.astype(jnp.bfloat16), log_total[..., 0])


def grad_band(query_head, grad_head, log_total, delta_head, key_head, value_head, allowed):
    scores = scores_for(query_head, key_head, allowed)
    probs = jnp.exp(scores - log_total[..., None])
    probs_low = probs.astype(jnp.bfloat16)
    prob_grad = jnp.einsum("tgd,kd->gtk", grad_head, value_head, preferred_element_type=jnp.float32)
    score_grad = (probs * (prob_grad - delta_head.T[..., None])).astype(jnp.bfloat16)
    query_part = (
        jnp.einsum("gtk,kd->tgd", score_grad, key_head, preferred_element_type=jnp.float32)
        * score_scale
    )
    key_part = (
        jnp.einsum("gtk,tgd->kd", score_grad, query_head, preferred_element_type=jnp.float32)
        * score_scale
    )
    value_part = jnp.einsum("gtk,tgd->kd", probs_low, grad_head, preferred_element_type=jnp.float32)
    return (query_part, key_part, value_part)


def device_body(rotated_queries, rotated_keys, value_matrix, out_grad, out_weight):
    tokens_dev = rotated_queries.shape[0]
    n_ctx = lax.axis_size(("cg", "cp"))
    kv_local = rotated_keys.shape[1] // HEAD_SIZE
    group_width = QUERY_HEAD_COUNT // KEY_VALUE_HEADS
    reach_count = WINDOW_SPAN // tokens_dev
    start_pos = lax.axis_index(("cg", "cp")) * tokens_dev
    query_pos = start_pos + jnp.arange(tokens_dev, dtype=jnp.int32)
    kv_width = rotated_keys.shape[1]
    own_pair = jnp.concatenate([rotated_keys, value_matrix], 1)
    earlier = [from_behind(own_pair, ("cg", "cp"), offset) for offset in range(reach_count, 0, -1)]
    pair_ext = jnp.concatenate(earlier + [own_pair], 0)
    key_ext = pair_ext[:, :kv_width]
    value_ext = pair_ext[:, kv_width:]
    key_pos = (
        start_pos
        - reach_count * tokens_dev
        + jnp.arange((reach_count + 1) * tokens_dev, dtype=jnp.int32)
    )
    full_mask = band_mask(query_pos, key_pos)
    query_heads = rotated_queries.reshape(tokens_dev, kv_local, group_width, HEAD_SIZE).transpose(
        1, 0, 2, 3
    )
    key_heads = key_ext.reshape(-1, kv_local, HEAD_SIZE).transpose(1, 0, 2)
    value_heads = value_ext.reshape(-1, kv_local, HEAD_SIZE).transpose(1, 0, 2)
    attn_heads, log_totals = lax.map(
        lambda items: forward_head(items[0], items[1], items[2], full_mask),
        (query_heads, key_heads, value_heads),
    )
    attn_rows = attn_heads.transpose(1, 0, 2, 3)
    attention_probs = attn_rows.reshape(tokens_dev, -1)
    partner_grad = lax.ppermute(out_grad, "tp", [(0, 1), (1, 0)])
    cotangent = jnp.where(
        lax.axis_index("tp") == 0,
        jnp.concatenate([out_grad, partner_grad], 1),
        jnp.concatenate([partner_grad, out_grad], 1),
    )
    group_size = lax.axis_size("cp")
    group_count = lax.axis_size("cg")
    block = cotangent.shape[1] // n_ctx
    weight_rows = out_weight.T
    group_weights = lax.all_to_all(
        jnp.broadcast_to(weight_rows, (group_size,) + weight_rows.shape), "cp", 0, 0, tiled=True
    ).reshape(group_size * block, -1)
    by_group = cotangent.reshape(tokens_dev, group_count, group_size * block).transpose(1, 0, 2)
    group_columns = lax.all_to_all(by_group, "cg", 0, 0, tiled=True)
    partial_grads = jnp.einsum(
        "btk,kh->bth", group_columns, group_weights, preferred_element_type=jnp.float32
    )
    grad_sum = jnp.sum(
        lax.all_to_all(partial_grads.astype(jnp.bfloat16), "cg", 0, 0, tiled=True).astype(
            jnp.float32
        ),
        0,
    )
    by_position = cotangent.reshape(tokens_dev, group_count, group_size, block).transpose(2, 0, 1, 3)
    by_position, grad_sum = lax.optimization_barrier((by_position, grad_sum))
    attention_gradient = grad_sum.astype(jnp.bfloat16)
    wg_columns = lax.all_to_all(by_position, "cp", 0, 0, tiled=True).reshape(
        group_size * tokens_dev, group_count, block
    )
    group_probs = lax.all_gather(attention_probs, "cp", axis=0, tiled=True)
    grad_rows = attention_gradient.reshape(tokens_dev, kv_local, group_width, HEAD_SIZE)
    row_deltas = jnp.sum(grad_rows.astype(jnp.float32) * attn_rows.astype(jnp.float32), axis=-1)
    head_gradients = grad_rows.transpose(1, 0, 2, 3)
    delta_heads = row_deltas.transpose(1, 0, 2)
    query_parts, key_parts, value_parts = lax.map(
        lambda items: grad_band(
            items[0], items[1], items[2], items[3], items[4], items[5], full_mask
        ),
        (query_heads, head_gradients, log_totals, delta_heads, key_heads, value_heads),
    )
    key_ext_grad = key_parts.transpose(1, 0, 2).reshape(-1, kv_local * HEAD_SIZE)
    value_ext_grad = value_parts.transpose(1, 0, 2).reshape(-1, kv_local * HEAD_SIZE)
    pair_grad = jnp.concatenate([key_ext_grad, value_ext_grad], 1)
    pair_total = pair_grad[reach_count * tokens_dev :]
    sent = [
        pair_grad[(reach_count - offset) * tokens_dev : (reach_count - offset + 1) * tokens_dev]
        for offset in range(1, reach_count + 1)
    ]
    sent = [block.astype(jnp.bfloat16) for block in sent]
    for offset in range(1, reach_count + 1):
        arrived = from_behind(sent[offset - 1], ("cg", "cp"), -offset)
        pair_total = pair_total + arrived.astype(jnp.float32)
    group_probs, wg_columns, sent = lax.optimization_barrier((group_probs, wg_columns, sent))
    weight_term = jnp.einsum(
        "th,tak->ahk", group_probs, wg_columns, preferred_element_type=jnp.float32
    ) * (tokens_dev * n_ctx) ** (-0.5)
    weight_parts = lax.all_to_all(weight_term.astype(jnp.bfloat16), "cg", 0, 0, tiled=True)
    weight_grad = jnp.sum(weight_parts.astype(jnp.float32), 0)
    key_total = pair_total[:, :kv_width]
    value_total = pair_total[:, kv_width:]
    query_grad = query_parts.transpose(1, 0, 2, 3).reshape(tokens_dev, -1).astype(jnp.bfloat16)
    return (
        query_grad,
        key_total.astype(jnp.bfloat16),
        value_total.astype(jnp.bfloat16),
        weight_grad,
    )


GROUP_SIZE = 8


def solution(mesh):
    n_ctx = mesh.shape["ctx"]
    group_size = GROUP_SIZE if n_ctx % GROUP_SIZE == 0 else 1
    devices = mesh.devices.reshape(n_ctx // group_size, group_size, mesh.shape["tp"])
    grouped = jax.sharding.Mesh(devices, ("cg", "cp", "tp"))
    ctx = ("cg", "cp")
    placed = (P(ctx, "tp"), P(ctx, "tp"), P(ctx, "tp"), P(ctx, "tp"), P("tp", ctx))
    return jax.shard_map(
        device_body,
        mesh=grouped,
        in_specs=placed,
        out_specs=(P(ctx, "tp"), P(ctx, "tp"), P(ctx, "tp"), P("tp", ctx)),
        check_vma=False,
    )
```

```python
import jax
import jax.numpy as jnp
from jax import lax
from jax.sharding import PartitionSpec as P


HEAD_SIZE = 128
WINDOW_SPAN = 1024
QUERY_HEAD_COUNT = 16
KEY_VALUE_HEADS = 8


score_scale = 168.0 ** (-0.5)


def from_behind(block, axis, distance):
    devices = range(lax.axis_size(axis))
    route = [(i - distance, i) for i in devices if i - distance in devices]
    return lax.ppermute(block, axis, route)


def band_mask(query_pos, key_pos):
    earlier = key_pos[None, :] <= query_pos[:, None]
    within = query_pos[:, None] - key_pos[None, :] < WINDOW_SPAN
    return earlier & within & (key_pos[None, :] >= 0)


def scores_for(query_head, key_head, allowed):
    scaled = (
        jnp.einsum("tgd,kd->gtk", query_head, key_head, preferred_element_type=jnp.float32)
        * score_scale
    )
    return jnp.where(allowed[None], scaled, -jnp.inf)


def forward_head(query_head, key_head, value_head, allowed):
    scores = scores_for(query_head, key_head, allowed)
    row_max = jnp.max(scores, axis=-1, keepdims=True)
    log_total = row_max + jnp.log(jnp.sum(jnp.exp(scores - row_max), axis=-1, keepdims=True))
    probs = jnp.exp(scores - log_total).astype(jnp.bfloat16)
    output = jnp.einsum("gtk,kd->tgd", probs, value_head, preferred_element_type=jnp.float32)
    return (output.astype(jnp.bfloat16), log_total[..., 0])


def grad_band(query_head, grad_head, log_total, delta_head, key_head, value_head, allowed):
    scores = scores_for(query_head, key_head, allowed)
    probs = jnp.exp(scores - log_total[..., None])
    probs_low = probs.astype(jnp.bfloat16)
    prob_grad = jnp.einsum("tgd,kd->gtk", grad_head, value_head, preferred_element_type=jnp.float32)
    score_grad = (probs * (prob_grad - delta_head.T[..., None])).astype(jnp.bfloat16)
    query_part = (
        jnp.einsum("gtk,kd->tgd", score_grad, key_head, preferred_element_type=jnp.float32)
        * score_scale
    )
    key_part = (
        jnp.einsum("gtk,tgd->kd", score_grad, query_head, preferred_element_type=jnp.float32)
        * score_scale
    )
    value_part = jnp.einsum("gtk,tgd->kd", probs_low, grad_head, preferred_element_type=jnp.float32)
    return (query_part, key_part, value_part)


def device_body(rotated_queries, rotated_keys, value_matrix, out_grad, out_weight):
    tokens_dev = rotated_queries.shape[0]
    n_ctx = lax.axis_size(("cg", "cp"))
    kv_local = rotated_keys.shape[1] // HEAD_SIZE
    group_width = QUERY_HEAD_COUNT // KEY_VALUE_HEADS
    reach_count = WINDOW_SPAN // tokens_dev
    start_pos = lax.axis_index(("cg", "cp")) * tokens_dev
    query_pos = start_pos + jnp.arange(tokens_dev, dtype=jnp.int32)
    kv_width = rotated_keys.shape[1]
    own_pair = jnp.concatenate([rotated_keys, value_matrix], 1)
    earlier = [from_behind(own_pair, ("cg", "cp"), offset) for offset in range(reach_count, 0, -1)]
    pair_ext = jnp.concatenate(earlier + [own_pair], 0)
    key_ext = pair_ext[:, :kv_width]
    value_ext = pair_ext[:, kv_width:]
    key_pos = (
        start_pos
        - reach_count * tokens_dev
        + jnp.arange((reach_count + 1) * tokens_dev, dtype=jnp.int32)
    )
    full_mask = band_mask(query_pos, key_pos)
    query_heads = rotated_queries.reshape(tokens_dev, kv_local, group_width, HEAD_SIZE).transpose(
        1, 0, 2, 3
    )
    key_heads = key_ext.reshape(-1, kv_local, HEAD_SIZE).transpose(1, 0, 2)
    value_heads = value_ext.reshape(-1, kv_local, HEAD_SIZE).transpose(1, 0, 2)
    attn_heads, log_totals = lax.map(
        lambda items: forward_head(items[0], items[1], items[2], full_mask),
        (query_heads, key_heads, value_heads),
    )
    attn_rows = attn_heads.transpose(1, 0, 2, 3)
    attention_probs = attn_rows.reshape(tokens_dev, -1)
    partner_grad = lax.ppermute(out_grad, "tp", [(0, 1), (1, 0)])
    cotangent = jnp.where(
        lax.axis_index("tp") == 0,
        jnp.concatenate([out_grad, partner_grad], 1),
        jnp.concatenate([partner_grad, out_grad], 1),
    )
    group_size = lax.axis_size("cp")
    group_count = lax.axis_size("cg")
    block = cotangent.shape[1] // n_ctx
    weight_rows = out_weight.T
    group_weights = lax.all_to_all(
        jnp.broadcast_to(weight_rows, (group_size,) + weight_rows.shape), "cp", 0, 0, tiled=True
    ).reshape(group_size * block, -1)
    by_group = cotangent.reshape(tokens_dev, group_count, group_size * block).transpose(1, 0, 2)
    group_columns = lax.all_to_all(by_group, "cg", 0, 0, tiled=True)
    partial_grads = jnp.einsum(
        "btk,kh->bth", group_columns, group_weights, preferred_element_type=jnp.float32
    )
    grad_sum = jnp.sum(
        lax.all_to_all(partial_grads.astype(jnp.bfloat16), "cg", 0, 0, tiled=True).astype(
            jnp.float32
        ),
        0,
    )
    attention_gradient = grad_sum.astype(jnp.bfloat16)
    group_probs = lax.all_gather(attention_probs, "cg", axis=0, tiled=True)
    grad_rows = attention_gradient.reshape(tokens_dev, kv_local, group_width, HEAD_SIZE)
    row_deltas = jnp.sum(grad_rows.astype(jnp.float32) * attn_rows.astype(jnp.float32), axis=-1)
    head_gradients = grad_rows.transpose(1, 0, 2, 3)
    delta_heads = row_deltas.transpose(1, 0, 2)
    query_parts, key_parts, value_parts = lax.map(
        lambda items: grad_band(
            items[0], items[1], items[2], items[3], items[4], items[5], full_mask
        ),
        (query_heads, head_gradients, log_totals, delta_heads, key_heads, value_heads),
    )
    key_ext_grad = key_parts.transpose(1, 0, 2).reshape(-1, kv_local * HEAD_SIZE)
    value_ext_grad = value_parts.transpose(1, 0, 2).reshape(-1, kv_local * HEAD_SIZE)
    pair_grad = jnp.concatenate([key_ext_grad, value_ext_grad], 1)
    ctx = ("cg", "cp")
    parts = [
        pair_grad[(reach_count - d) * tokens_dev : (reach_count - d + 1) * tokens_dev]
        for d in range(reach_count + 1)
    ]
    width = reach_count
    arrived = from_behind(parts[width].astype(jnp.bfloat16), ctx, -1)
    parts = parts[:width]
    parts[width - 1] = parts[width - 1] + arrived.astype(jnp.float32)
    sent = arrived
    assert width & (width - 1) == 0
    while width > 1:
        half = width // 2
        moved = from_behind(jnp.stack(parts[half:]).astype(jnp.bfloat16), ctx, -half)
        parts = [parts[k] + moved[k].astype(jnp.float32) for k in range(half)]
        width = half
    pair_total = parts[0]
    group_probs, group_columns, sent = lax.optimization_barrier((group_probs, group_columns, sent))
    weight_term = jnp.einsum(
        "th,tqk->qhk",
        group_probs,
        group_columns.reshape(group_count * tokens_dev, group_size, block),
        preferred_element_type=jnp.float32,
    ) * (tokens_dev * n_ctx) ** (-0.5)
    weight_parts = lax.all_to_all(weight_term.astype(jnp.bfloat16), "cp", 0, 0, tiled=True)
    weight_grad = jnp.sum(weight_parts.astype(jnp.float32), 0)
    key_total = pair_total[:, :kv_width]
    value_total = pair_total[:, kv_width:]
    query_grad = query_parts.transpose(1, 0, 2, 3).reshape(tokens_dev, -1).astype(jnp.bfloat16)
    return (
        query_grad,
        key_total.astype(jnp.bfloat16),
        value_total.astype(jnp.bfloat16),
        weight_grad,
    )


GROUP_SIZE = 8


def solution(mesh):
    n_ctx = mesh.shape["ctx"]
    group_size = GROUP_SIZE if n_ctx % GROUP_SIZE == 0 else 1
    devices = mesh.devices.reshape(n_ctx // group_size, group_size, mesh.shape["tp"])
    grouped = jax.sharding.Mesh(devices, ("cg", "cp", "tp"))
    ctx = ("cg", "cp")
    placed = (P(ctx, "tp"), P(ctx, "tp"), P(ctx, "tp"), P(ctx, "tp"), P("tp", ctx))
    return jax.shard_map(
        device_body,
        mesh=grouped,
        in_specs=placed,
        out_specs=(P(ctx, "tp"), P(ctx, "tp"), P(ctx, "tp"), P("tp", ctx)),
        check_vma=False,
    )
```

```python
import jax
import jax.numpy as jnp
from jax import lax
from jax.sharding import PartitionSpec as P


HEAD_SIZE = 128
WINDOW_SPAN = 1024
QUERY_HEAD_COUNT = 16
KEY_VALUE_HEADS = 8


score_scale = 168.0 ** (-0.5)


def from_behind(block, axis, distance):
    devices = range(lax.axis_size(axis))
    route = [(i - distance, i) for i in devices if i - distance in devices]
    return lax.ppermute(block, axis, route)


def band_mask(query_pos, key_pos):
    earlier = key_pos[None, :] <= query_pos[:, None]
    within = query_pos[:, None] - key_pos[None, :] < WINDOW_SPAN
    return earlier & within & (key_pos[None, :] >= 0)


def scores_for(query_head, key_head, allowed):
    scaled = (
        jnp.einsum("tgd,kd->gtk", query_head, key_head, preferred_element_type=jnp.float32)
        * score_scale
    )
    return jnp.where(allowed[None], scaled, -jnp.inf)


def forward_head(query_head, key_head, value_head, allowed):
    scores = scores_for(query_head, key_head, allowed)
    row_max = jnp.max(scores, axis=-1, keepdims=True)
    log_total = row_max + jnp.log(jnp.sum(jnp.exp(scores - row_max), axis=-1, keepdims=True))
    probs = jnp.exp(scores - log_total).astype(jnp.bfloat16)
    output = jnp.einsum("gtk,kd->tgd", probs, value_head, preferred_element_type=jnp.float32)
    return (output.astype(jnp.bfloat16), log_total[..., 0])


def grad_band(query_head, grad_head, log_total, delta_head, key_head, value_head, allowed):
    scores = scores_for(query_head, key_head, allowed)
    probs = jnp.exp(scores - log_total[..., None])
    probs_low = probs.astype(jnp.bfloat16)
    prob_grad = jnp.einsum("tgd,kd->gtk", grad_head, value_head, preferred_element_type=jnp.float32)
    score_grad = (probs * (prob_grad - delta_head.T[..., None])).astype(jnp.bfloat16)
    query_part = (
        jnp.einsum("gtk,kd->tgd", score_grad, key_head, preferred_element_type=jnp.float32)
        * score_scale
    )
    key_part = (
        jnp.einsum("gtk,tgd->kd", score_grad, query_head, preferred_element_type=jnp.float32)
        * score_scale
    )
    value_part = jnp.einsum("gtk,tgd->kd", probs_low, grad_head, preferred_element_type=jnp.float32)
    return (query_part, key_part, value_part)


def device_body(rotated_queries, rotated_keys, value_matrix, out_grad, out_weight):
    tokens_dev = rotated_queries.shape[0]
    n_ctx = lax.axis_size(("cg", "cp"))
    kv_local = rotated_keys.shape[1] // HEAD_SIZE
    group_width = QUERY_HEAD_COUNT // KEY_VALUE_HEADS
    reach_count = WINDOW_SPAN // tokens_dev
    start_pos = lax.axis_index(("cg", "cp")) * tokens_dev
    query_pos = start_pos + jnp.arange(tokens_dev, dtype=jnp.int32)
    kv_width = rotated_keys.shape[1]
    own_pair = jnp.concatenate([rotated_keys, value_matrix], 1)
    earlier = [from_behind(own_pair, ("cg", "cp"), offset) for offset in range(reach_count, 0, -1)]
    pair_ext = jnp.concatenate(earlier + [own_pair], 0)
    key_ext = pair_ext[:, :kv_width]
    value_ext = pair_ext[:, kv_width:]
    key_pos = (
        start_pos
        - reach_count * tokens_dev
        + jnp.arange((reach_count + 1) * tokens_dev, dtype=jnp.int32)
    )
    full_mask = band_mask(query_pos, key_pos)
    query_heads = rotated_queries.reshape(tokens_dev, kv_local, group_width, HEAD_SIZE).transpose(
        1, 0, 2, 3
    )
    key_heads = key_ext.reshape(-1, kv_local, HEAD_SIZE).transpose(1, 0, 2)
    value_heads = value_ext.reshape(-1, kv_local, HEAD_SIZE).transpose(1, 0, 2)
    attn_heads, log_totals = lax.map(
        lambda items: forward_head(items[0], items[1], items[2], full_mask),
        (query_heads, key_heads, value_heads),
    )
    attn_rows = attn_heads.transpose(1, 0, 2, 3)
    attention_probs = attn_rows.reshape(tokens_dev, -1)
    partner_grad = lax.ppermute(out_grad, "tp", [(0, 1), (1, 0)])
    cotangent = jnp.where(
        lax.axis_index("tp") == 0,
        jnp.concatenate([out_grad, partner_grad], 1),
        jnp.concatenate([partner_grad, out_grad], 1),
    )
    group_size = lax.axis_size("cp")
    group_count = lax.axis_size("cg")
    block = cotangent.shape[1] // n_ctx
    weight_rows = out_weight.T
    group_weights = lax.all_to_all(
        jnp.broadcast_to(weight_rows, (group_size,) + weight_rows.shape), "cp", 0, 0, tiled=True
    ).reshape(group_size * block, -1)
    by_group = cotangent.reshape(tokens_dev, group_count, group_size * block).transpose(1, 0, 2)
    group_columns = lax.all_to_all(by_group, "cg", 0, 0, tiled=True)
    partial_grads = jnp.einsum(
        "btk,kh->bth", group_columns, group_weights, preferred_element_type=jnp.float32
    )
    grad_sum = jnp.sum(
        lax.all_to_all(partial_grads.astype(jnp.bfloat16), "cg", 0, 0, tiled=True).astype(
            jnp.float32
        ),
        0,
    )
    attention_gradient = grad_sum.astype(jnp.bfloat16)
    group_probs = lax.all_gather(attention_probs, "cg", axis=0, tiled=True)
    grad_rows = attention_gradient.reshape(tokens_dev, kv_local, group_width, HEAD_SIZE)
    row_deltas = jnp.sum(grad_rows.astype(jnp.float32) * attn_rows.astype(jnp.float32), axis=-1)
    head_gradients = grad_rows.transpose(1, 0, 2, 3)
    delta_heads = row_deltas.transpose(1, 0, 2)
    query_parts, key_parts, value_parts = lax.map(
        lambda items: grad_band(
            items[0], items[1], items[2], items[3], items[4], items[5], full_mask
        ),
        (query_heads, head_gradients, log_totals, delta_heads, key_heads, value_heads),
    )
    key_ext_grad = key_parts.transpose(1, 0, 2).reshape(-1, kv_local * HEAD_SIZE)
    value_ext_grad = value_parts.transpose(1, 0, 2).reshape(-1, kv_local * HEAD_SIZE)
    pair_grad = jnp.concatenate([key_ext_grad, value_ext_grad], 1)
    pair_total = pair_grad[reach_count * tokens_dev :]
    sent = [
        pair_grad[(reach_count - offset) * tokens_dev : (reach_count - offset + 1) * tokens_dev]
        for offset in range(1, reach_count + 1)
    ]
    sent = [block.astype(jnp.bfloat16) for block in sent]
    for offset in range(1, reach_count + 1):
        arrived = from_behind(sent[offset - 1], ("cg", "cp"), -offset)
        pair_total = pair_total + arrived.astype(jnp.float32)
    group_probs, group_columns, sent = lax.optimization_barrier((group_probs, group_columns, sent))
    weight_term = jnp.einsum(
        "th,tqk->qhk",
        group_probs,
        group_columns.reshape(group_count * tokens_dev, group_size, block),
        preferred_element_type=jnp.float32,
    ) * (tokens_dev * n_ctx) ** (-0.5)
    weight_grad = lax.psum_scatter(weight_term, "cp", scatter_dimension=0, tiled=True)[0]
    key_total = pair_total[:, :kv_width]
    value_total = pair_total[:, kv_width:]
    query_grad = query_parts.transpose(1, 0, 2, 3).reshape(tokens_dev, -1).astype(jnp.bfloat16)
    return (
        query_grad,
        key_total.astype(jnp.bfloat16),
        value_total.astype(jnp.bfloat16),
        weight_grad,
    )


GROUP_SIZE = 8


def solution(mesh):
    n_ctx = mesh.shape["ctx"]
    group_size = GROUP_SIZE if n_ctx % GROUP_SIZE == 0 else 1
    devices = mesh.devices.reshape(n_ctx // group_size, group_size, mesh.shape["tp"])
    grouped = jax.sharding.Mesh(devices, ("cg", "cp", "tp"))
    ctx = ("cg", "cp")
    placed = (P(ctx, "tp"), P(ctx, "tp"), P(ctx, "tp"), P(ctx, "tp"), P("tp", ctx))
    return jax.shard_map(
        device_body,
        mesh=grouped,
        in_specs=placed,
        out_specs=(P(ctx, "tp"), P(ctx, "tp"), P(ctx, "tp"), P("tp", ctx)),
        check_vma=False,
    )
```

```python
import jax
import jax.numpy as jnp
from jax import lax
from jax.sharding import PartitionSpec as P


HEAD_SIZE = 128
WINDOW_SPAN = 1024
QUERY_HEAD_COUNT = 16
KEY_VALUE_HEADS = 8


score_scale = 168.0 ** (-0.5)


def from_behind(block, axis, distance):
    devices = range(lax.axis_size(axis))
    route = [(i - distance, i) for i in devices if i - distance in devices]
    return lax.ppermute(block, axis, route)


def band_mask(query_pos, key_pos):
    earlier = key_pos[None, :] <= query_pos[:, None]
    within = query_pos[:, None] - key_pos[None, :] < WINDOW_SPAN
    return earlier & within & (key_pos[None, :] >= 0)


def scores_for(query_head, key_head, allowed):
    scaled = (
        jnp.einsum("tgd,kd->gtk", query_head, key_head, preferred_element_type=jnp.float32)
        * score_scale
    )
    return jnp.where(allowed[None], scaled, -jnp.inf)


def forward_head(query_head, key_head, value_head, allowed):
    scores = scores_for(query_head, key_head, allowed)
    row_max = jnp.max(scores, axis=-1, keepdims=True)
    log_total = row_max + jnp.log(jnp.sum(jnp.exp(scores - row_max), axis=-1, keepdims=True))
    probs = jnp.exp(scores - log_total).astype(jnp.bfloat16)
    output = jnp.einsum("gtk,kd->tgd", probs, value_head, preferred_element_type=jnp.float32)
    return (output.astype(jnp.bfloat16), log_total[..., 0])


def grad_band(query_head, grad_head, log_total, delta_head, key_head, value_head, allowed):
    scores = scores_for(query_head, key_head, allowed)
    probs = jnp.exp(scores - log_total[..., None])
    probs_low = probs.astype(jnp.bfloat16)
    prob_grad = jnp.einsum("tgd,kd->gtk", grad_head, value_head, preferred_element_type=jnp.float32)
    score_grad = (probs * (prob_grad - delta_head.T[..., None])).astype(jnp.bfloat16)
    query_part = (
        jnp.einsum("gtk,kd->tgd", score_grad, key_head, preferred_element_type=jnp.float32)
        * score_scale
    )
    key_part = (
        jnp.einsum("gtk,tgd->kd", score_grad, query_head, preferred_element_type=jnp.float32)
        * score_scale
    )
    value_part = jnp.einsum("gtk,tgd->kd", probs_low, grad_head, preferred_element_type=jnp.float32)
    return (query_part, key_part, value_part)


def device_body(rotated_queries, rotated_keys, value_matrix, out_grad, out_weight):
    tokens_dev = rotated_queries.shape[0]
    n_ctx = lax.axis_size(("cg", "cp"))
    kv_local = rotated_keys.shape[1] // HEAD_SIZE
    group_width = QUERY_HEAD_COUNT // KEY_VALUE_HEADS
    reach_count = WINDOW_SPAN // tokens_dev
    start_pos = lax.axis_index(("cg", "cp")) * tokens_dev
    query_pos = start_pos + jnp.arange(tokens_dev, dtype=jnp.int32)
    kv_width = rotated_keys.shape[1]
    own_pair = jnp.concatenate([rotated_keys, value_matrix], 1)
    earlier = [from_behind(own_pair, ("cg", "cp"), offset) for offset in range(reach_count, 0, -1)]
    pair_ext = jnp.concatenate(earlier + [own_pair], 0)
    key_ext = pair_ext[:, :kv_width]
    value_ext = pair_ext[:, kv_width:]
    key_pos = (
        start_pos
        - reach_count * tokens_dev
        + jnp.arange((reach_count + 1) * tokens_dev, dtype=jnp.int32)
    )
    full_mask = band_mask(query_pos, key_pos)
    query_heads = rotated_queries.reshape(tokens_dev, kv_local, group_width, HEAD_SIZE).transpose(
        1, 0, 2, 3
    )
    key_heads = key_ext.reshape(-1, kv_local, HEAD_SIZE).transpose(1, 0, 2)
    value_heads = value_ext.reshape(-1, kv_local, HEAD_SIZE).transpose(1, 0, 2)
    attn_heads, log_totals = lax.map(
        lambda items: forward_head(items[0], items[1], items[2], full_mask),
        (query_heads, key_heads, value_heads),
    )
    attn_rows = attn_heads.transpose(1, 0, 2, 3)
    attention_probs = attn_rows.reshape(tokens_dev, -1)
    partner_grad = lax.ppermute(out_grad, "tp", [(0, 1), (1, 0)])
    cotangent = jnp.where(
        lax.axis_index("tp") == 0,
        jnp.concatenate([out_grad, partner_grad], 1),
        jnp.concatenate([partner_grad, out_grad], 1),
    )
    group_size = lax.axis_size("cp")
    group_count = lax.axis_size("cg")
    block = cotangent.shape[1] // n_ctx
    weight_rows = out_weight.T
    group_weights = lax.all_to_all(
        jnp.broadcast_to(weight_rows, (group_size,) + weight_rows.shape), "cp", 0, 0, tiled=True
    ).reshape(group_size * block, -1)
    by_group = cotangent.reshape(tokens_dev, group_count, group_size * block).transpose(1, 0, 2)
    group_columns = lax.all_to_all(by_group, "cg", 0, 0, tiled=True)
    partial_grads = jnp.einsum(
        "btk,kh->bth", group_columns, group_weights, preferred_element_type=jnp.float32
    )
    grad_sum = jnp.sum(
        lax.all_to_all(partial_grads.astype(jnp.bfloat16), "cg", 0, 0, tiled=True).astype(
            jnp.float32
        ),
        0,
    )
    attention_gradient = grad_sum.astype(jnp.bfloat16)
    group_probs = lax.all_gather(attention_probs, "cg", axis=0, tiled=True)
    grad_rows = attention_gradient.reshape(tokens_dev, kv_local, group_width, HEAD_SIZE)
    row_deltas = jnp.sum(grad_rows.astype(jnp.float32) * attn_rows.astype(jnp.float32), axis=-1)
    head_gradients = grad_rows.transpose(1, 0, 2, 3)
    delta_heads = row_deltas.transpose(1, 0, 2)
    query_parts, key_parts, value_parts = lax.map(
        lambda items: grad_band(
            items[0], items[1], items[2], items[3], items[4], items[5], full_mask
        ),
        (query_heads, head_gradients, log_totals, delta_heads, key_heads, value_heads),
    )
    key_ext_grad = key_parts.transpose(1, 0, 2).reshape(-1, kv_local * HEAD_SIZE)
    value_ext_grad = value_parts.transpose(1, 0, 2).reshape(-1, kv_local * HEAD_SIZE)
    pair_grad = jnp.concatenate([key_ext_grad, value_ext_grad], 1)
    pair_total = pair_grad[reach_count * tokens_dev :]
    sent = [
        pair_grad[(reach_count - offset) * tokens_dev : (reach_count - offset + 1) * tokens_dev]
        for offset in range(1, reach_count + 1)
    ]
    sent = [block.astype(jnp.bfloat16) for block in sent]
    for offset in range(reach_count, 0, -1):
        arrived = from_behind(sent[offset - 1], ("cg", "cp"), -offset)
        pair_total = pair_total + arrived.astype(jnp.float32)
    group_probs, group_columns, sent = lax.optimization_barrier((group_probs, group_columns, sent))
    weight_term = jnp.einsum(
        "th,tqk->qhk",
        group_probs,
        group_columns.reshape(group_count * tokens_dev, group_size, block),
        preferred_element_type=jnp.float32,
    ) * (tokens_dev * n_ctx) ** (-0.5)
    weight_parts = lax.all_to_all(weight_term.astype(jnp.bfloat16), "cp", 0, 0, tiled=True)
    weight_grad = jnp.sum(weight_parts.astype(jnp.float32), 0)
    key_total = pair_total[:, :kv_width]
    value_total = pair_total[:, kv_width:]
    query_grad = query_parts.transpose(1, 0, 2, 3).reshape(tokens_dev, -1).astype(jnp.bfloat16)
    return (
        query_grad,
        key_total.astype(jnp.bfloat16),
        value_total.astype(jnp.bfloat16),
        weight_grad,
    )


GROUP_SIZE = 8


def solution(mesh):
    n_ctx = mesh.shape["ctx"]
    group_size = GROUP_SIZE if n_ctx % GROUP_SIZE == 0 else 1
    devices = mesh.devices.reshape(n_ctx // group_size, group_size, mesh.shape["tp"])
    grouped = jax.sharding.Mesh(devices, ("cg", "cp", "tp"))
    ctx = ("cg", "cp")
    placed = (P(ctx, "tp"), P(ctx, "tp"), P(ctx, "tp"), P(ctx, "tp"), P("tp", ctx))
    return jax.shard_map(
        device_body,
        mesh=grouped,
        in_specs=placed,
        out_specs=(P(ctx, "tp"), P(ctx, "tp"), P(ctx, "tp"), P("tp", ctx)),
        check_vma=False,
    )
```
